128 devices in a mesh: chan: 8 (over x, core), tm: 16 (over z, y).
Axes of the slice: x: 4, y: 4, z: 4, core: 2. Of those that a mesh axis runs over, the one named last changes fastest.
Arguments:
- voltages: bfloat16 [128, 8192, 2, 512], P('tm', 'chan'), may hold values from -8 to 8
- window_stations: int32 [2], replicated, may hold values from 0 to 255
- channel_flags: int32 [8192], replicated, may hold values 0 or 1
Outputs:
- rm_spectrum: float32 [16, 16, 2, 2, 1024], P('tm', 'chan')
- leakage: float32 [2, 256], replicated
The draws below stay inside these ranges and needn't reach their ends.
All inputs are finite; a program needn't handle non-finite values.
Results may differ from the reference program's by a relative error of at most 0.012.
Values may be sent and summed in bfloat16 or wider, within the bound.
No kernel may reach another device: no remote copies, remote signals or barrier semaphores. Data moves between devices by JAX's collectives and lax.ppermute only.
A program may use at most 128 MiB of HBM per device.

```python
import math
import jax
import jax.numpy as jnp
from jax import lax

STATIONS = 256
CHANNELS = 8192
DEPTH = 1024
WINDOW = 2
TIME_DEV = 8
ITERATIONS = 3
TIME = 128
N_TM = 16


def draw_voltages(key, part):
    first, second, third = jax.random.split(key, 3)
    shape = (TIME, CHANNELS, 2, STATIONS)
    signal = jax.random.normal(first, shape, jnp.float32)
    noise = jax.random.normal(second, shape, jnp.float32)
    gain = jnp.exp(jax.random.uniform(third, (1, CHANNELS, 1, STATIONS), jnp.float32, -0.5, 0.5))
    first_feed = signal * gain
    second_feed = (0.6 * signal + 0.8 * noise) * gain
    both = jnp.stack([first_feed, second_feed], -1).reshape(TIME, CHANNELS, 2, 2 * STATIONS)
    return jnp.clip(both, -8.0, 8.0).astype(jnp.bfloat16)


def touch_ends(result, own_key, least, top_value):
    place = [jax.random.randint(jax.random.fold_in(own_key, axis), (), 0, length) for axis, length in enumerate(result.shape)]
    longest = result.shape.index(max(result.shape))
    next_to = place[:longest] + [(place[longest] + 1) % result.shape[longest]] + place[longest + 1:]
    return result.at[tuple(place)].set(least).at[tuple(next_to)].set(top_value)


def setup_inputs(seed: int = 0) -> dict:
    streams_of = jax.random.split(jax.random.key(seed), 4)
    voltages = draw_voltages(jax.random.fold_in(streams_of[3], 71), 0)
    window_stations = jax.random.randint(streams_of[1], (WINDOW,), 0, STATIONS).astype(jnp.int32)
    channel_flags = touch_ends((jax.random.randint(streams_of[2], (CHANNELS,), 0, 8) < 7).astype(jnp.int32), jax.random.fold_in(streams_of[2], 1), 0, 1)
    return {"voltages": voltages, "window_stations": window_stations, "channel_flags": channel_flags}


def phase_table(first_channel, channel_count):
    chan_pos = (first_channel + jnp.arange(channel_count)).astype(jnp.float32)
    frequency = 1.0 + (chan_pos + 0.5) / CHANNELS
    lambda_sq = 1.0 / (frequency * frequency)
    depth_grid = (jnp.arange(DEPTH).astype(jnp.float32) - DEPTH // 2) * 2.0
    angles = 2.0 * depth_grid[None, :] * (lambda_sq[:, None] - 0.5)
    return (jnp.cos(angles).astype(jnp.bfloat16), jnp.sin(angles).astype(jnp.bfloat16))

def station_terms(leak_real, leak_imag, fields, station_map, window_map):
    far_real = lax.optimization_barrier(jnp.sum(station_map * leak_real[None, :], 1))[:, None]
    far_imag = lax.optimization_barrier(jnp.sum(station_map * leak_imag[None, :], 1))[:, None]
    near_real = lax.optimization_barrier(jnp.sum(window_map * leak_real[None, :], 1))[None, :]
    near_imag = lax.optimization_barrier(jnp.sum(window_map * leak_imag[None, :], 1))[None, :]
    row_real = fields[0] - (far_real * fields[2] + far_imag * fields[3])
    row_imag = fields[1] - (far_real * fields[3] - far_imag * fields[2])
    col_real = fields[4] - (near_real * fields[2] + near_imag * fields[3])
    col_imag = -(fields[5] - (near_imag * fields[2] - near_real * fields[3]))
    numer_real = lax.optimization_barrier(jnp.sum(window_map * lax.optimization_barrier(jnp.sum(row_real, 0))[:, None], 0)) + lax.optimization_barrier(jnp.sum(station_map * lax.optimization_barrier(jnp.sum(col_real, 1))[:, None], 0))
    numer_imag = lax.optimization_barrier(jnp.sum(window_map * lax.optimization_barrier(jnp.sum(row_imag, 0))[:, None], 0)) + lax.optimization_barrier(jnp.sum(station_map * lax.optimization_barrier(jnp.sum(col_imag, 1))[:, None], 0))
    weight_sum = lax.optimization_barrier(jnp.sum(window_map * lax.optimization_barrier(jnp.sum(fields[6], 0))[:, None], 0)) + lax.optimization_barrier(jnp.sum(station_map * lax.optimization_barrier(jnp.sum(fields[7], 1))[:, None], 0))
    return (numer_real, numer_imag, weight_sum)

def reference(voltages, window_stations, channel_flags):
    feed_index = (2 * window_stations[:, None] + jnp.arange(2, dtype=jnp.int32)[None, :]).reshape(-1).astype(jnp.int32)

    def add_shard(shard, total):
        block = lax.dynamic_slice_in_dim(voltages, shard * TIME_DEV, TIME_DEV, 0).astype(jnp.float32)
        picked = jnp.take(block, feed_index, axis=3)
        blocks = jnp.einsum('tcaw,tcbx->cbawx', picked, block, precision=lax.Precision.HIGHEST)
        real_part = blocks[:, 0, 0] + blocks[:, 1, 1]
        imag_part = blocks[:, 0, 1] - blocks[:, 1, 0]
        rounded = lax.optimization_barrier(jnp.stack([real_part, imag_part], 1).astype(jnp.bfloat16))
        return total + rounded.astype(jnp.float32)
    total = lax.fori_loop(0, N_TM, add_shard, jnp.zeros((CHANNELS, 2, 2 * WINDOW, 2 * STATIONS), jnp.float32))
    stored = lax.optimization_barrier(total.astype(jnp.bfloat16))
    six = stored.astype(jnp.float32).reshape(CHANNELS, 2, WINDOW, 2, STATIONS, 2)

    def correlation(feed_a, feed_b):
        return jnp.transpose(six[:, :, :, feed_a, :, feed_b], (1, 3, 2, 0))
    corr_xx = correlation(0, 0)
    corr_xy = correlation(0, 1)
    corr_yx = correlation(1, 0)
    corr_yy = correlation(1, 1)
    flag_weights = channel_flags.astype(jnp.float32)
    pol_real = 0.5 * (corr_xx[0] - corr_yy[0]) - 0.5 * (corr_xy[1] + corr_yx[1])
    pol_imag = 0.5 * (corr_xx[1] - corr_yy[1]) + 0.5 * (corr_xy[0] + corr_yx[0])
    pol_real = (pol_real * flag_weights).astype(jnp.bfloat16).reshape(STATIONS * WINDOW, CHANNELS)
    pol_imag = (pol_imag * flag_weights).astype(jnp.bfloat16).reshape(STATIONS * WINDOW, CHANNELS)
    cosine, sine_part = phase_table(0, CHANNELS)
    out_real = jnp.dot(pol_real, cosine, preferred_element_type=jnp.float32) + jnp.dot(pol_imag, sine_part, preferred_element_type=jnp.float32)
    out_imag = jnp.dot(pol_imag, cosine, preferred_element_type=jnp.float32) - jnp.dot(pol_real, sine_part, preferred_element_type=jnp.float32)
    norm_factor = 1.0 / math.sqrt(CHANNELS * TIME)
    spectrum = jnp.stack([out_real, out_imag], 1) * norm_factor
    rm_spectrum = spectrum.reshape(N_TM, STATIONS // N_TM, WINDOW, 2, DEPTH)

    def conj_sum(left, right):
        real_part = lax.optimization_barrier(jnp.sum(flag_weights * (left[0] * right[0] + left[1] * right[1]), -1)) / CHANNELS
        imag_part = lax.optimization_barrier(jnp.sum(flag_weights * (left[1] * right[0] - left[0] * right[1]), -1)) / CHANNELS
        return (real_part, imag_part)
    cross_real, cross_imag = conj_sum(corr_xy, corr_yy)
    mixed_real, mixed_imag = conj_sum(corr_xx, corr_yy)
    side_real, side_imag = conj_sum(corr_xy, corr_xx)
    power_y = lax.optimization_barrier(jnp.sum(flag_weights * (corr_yy[0] * corr_yy[0] + corr_yy[1] * corr_yy[1]), -1)) / CHANNELS
    power_x = lax.optimization_barrier(jnp.sum(flag_weights * (corr_xx[0] * corr_xx[0] + corr_xx[1] * corr_xx[1]), -1)) / CHANNELS
    fields = [cross_real, cross_imag, mixed_real, mixed_imag, side_real, side_imag, power_y, power_x]
    station_axis = jnp.arange(STATIONS, dtype=jnp.int32)
    window_map = (window_stations[:, None] == station_axis[None, :]).astype(jnp.float32)
    station_map = jnp.eye(STATIONS, dtype=jnp.float32)
    leak_real = jnp.zeros((STATIONS,), jnp.float32)
    leak_imag = jnp.zeros((STATIONS,), jnp.float32)
    for iteration in range(ITERATIONS):
        numer_real, numer_imag, weight_sum = station_terms(leak_real, leak_imag, fields, station_map, window_map)
        leak_real = numer_real / (weight_sum + 1e-06)
        leak_imag = numer_imag / (weight_sum + 1e-06)
    return (rm_spectrum, jnp.stack([leak_real, leak_imag], 0))
```

```python
import math

import jax
import jax.numpy as jnp
from jax import lax
from jax.sharding import PartitionSpec as P

CHANNELS = 8192
DEPTH = 1024
ITERATIONS = 3


def phase_table(first_channel, channel_count):
    chan_pos = (first_channel + jnp.arange(channel_count, dtype=jnp.int32)).astype(jnp.float32)
    frequency = 1.0 + (chan_pos + 0.5) / CHANNELS
    lambda_sq = 1.0 / (frequency * frequency)
    depth_grid = (jnp.arange(DEPTH).astype(jnp.float32) - DEPTH // 2) * 2.0
    angles = 2.0 * depth_grid[None, :] * (lambda_sq[:, None] - 0.5)
    return (jnp.cos(angles).astype(jnp.bfloat16), jnp.sin(angles).astype(jnp.bfloat16))


def station_terms(leak_real, leak_imag, fields, station_map, window_map):
    far_real = jnp.sum(station_map * leak_real[None, :], 1)[:, None]
    far_imag = jnp.sum(station_map * leak_imag[None, :], 1)[:, None]
    near_real = jnp.sum(window_map * leak_real[None, :], 1)[None, :]
    near_imag = jnp.sum(window_map * leak_imag[None, :], 1)[None, :]
    row_real = fields[0] - (far_real * fields[2] + far_imag * fields[3])
    row_imag = fields[1] - (far_real * fields[3] - far_imag * fields[2])
    col_real = fields[4] - (near_real * fields[2] + near_imag * fields[3])
    col_imag = -(fields[5] - (near_imag * fields[2] - near_real * fields[3]))
    numer_real = jnp.sum(window_map * jnp.sum(row_real, 0)[:, None], 0) + jnp.sum(
        station_map * jnp.sum(col_real, 1)[:, None], 0
    )
    numer_imag = jnp.sum(window_map * jnp.sum(row_imag, 0)[:, None], 0) + jnp.sum(
        station_map * jnp.sum(col_imag, 1)[:, None], 0
    )
    weight_sum = jnp.sum(window_map * jnp.sum(fields[6], 0)[:, None], 0) + jnp.sum(
        station_map * jnp.sum(fields[7], 1)[:, None], 0
    )
    return (numer_real, numer_imag, weight_sum)


def spectrum_terms(local_vis, first_channel, flag_weights):
    pairs = local_vis.shape[0] // 2
    window = local_vis.shape[2] // 2
    channel_count = local_vis.shape[3]
    six = local_vis.reshape(pairs, 2, 2, window, 2, channel_count)

    def correlation(feed_a, feed_b):
        return six[:, feed_b, :, :, feed_a, :].astype(jnp.float32)

    corr_xx = correlation(0, 0)
    corr_xy = correlation(0, 1)
    corr_yx = correlation(1, 0)
    corr_yy = correlation(1, 1)
    pol_real = 0.5 * (corr_xx[:, 0] - corr_yy[:, 0]) - 0.5 * (corr_xy[:, 1] + corr_yx[:, 1])
    pol_imag = 0.5 * (corr_xx[:, 1] - corr_yy[:, 1]) + 0.5 * (corr_xy[:, 0] + corr_yx[:, 0])
    pol_real = (pol_real * flag_weights).astype(jnp.bfloat16).reshape(pairs * window, channel_count)
    pol_imag = (pol_imag * flag_weights).astype(jnp.bfloat16).reshape(pairs * window, channel_count)

    def conj_sum(left, right):
        real_part = jnp.sum(
            flag_weights * (left[:, 0] * right[:, 0] + left[:, 1] * right[:, 1]), -1
        )
        imag_part = jnp.sum(
            flag_weights * (left[:, 1] * right[:, 0] - left[:, 0] * right[:, 1]), -1
        )
        return (real_part, imag_part)

    cross_real, cross_imag = conj_sum(corr_xy, corr_yy)
    mixed_real, mixed_imag = conj_sum(corr_xx, corr_yy)
    side_real, side_imag = conj_sum(corr_xy, corr_xx)
    power_y = jnp.sum(
        flag_weights * (corr_yy[:, 0] * corr_yy[:, 0] + corr_yy[:, 1] * corr_yy[:, 1]), -1
    )
    power_x = jnp.sum(
        flag_weights * (corr_xx[:, 0] * corr_xx[:, 0] + corr_xx[:, 1] * corr_xx[:, 1]), -1
    )
    baseline_stats = jnp.stack(
        [cross_real, cross_imag, mixed_real, mixed_imag, side_real, side_imag, power_y, power_x], -1
    )
    block_width = math.gcd(channel_count, 1024)

    def add_block(block_id, total):
        offset = block_id * block_width
        cosine, sine_part = phase_table(first_channel + offset, block_width)
        left = jnp.concatenate(
            [
                lax.dynamic_slice_in_dim(pol_real, offset, block_width, 1),
                lax.dynamic_slice_in_dim(pol_imag, offset, block_width, 1),
            ],
            1,
        )
        right = jnp.concatenate(
            [jnp.concatenate([cosine, -sine_part], 1), jnp.concatenate([sine_part, cosine], 1)], 0
        )
        return total + jnp.dot(left, right, preferred_element_type=jnp.float32)

    total = lax.fori_loop(
        0,
        channel_count // block_width,
        add_block,
        jnp.zeros((pairs * window, 2 * DEPTH), jnp.float32),
    )
    return (total.reshape(pairs, window, 2 * DEPTH), baseline_stats)


def per_device(voltages, window_stations, channel_flags):
    tm_size = lax.axis_size("tm")
    chan_size = lax.axis_size("chan")
    inputs = voltages.shape[3]
    stations = inputs // 2
    window = window_stations.shape[0]
    channel_count = voltages.shape[1]
    feed_index = (2 * window_stations[:, None] + jnp.arange(2, dtype=jnp.int32)[None, :]).reshape(
        -1
    )
    picked = jnp.take(voltages, feed_index, axis=3)
    blocks = jnp.einsum("tcaw,tcbx->xbawc", picked, voltages, preferred_element_type=jnp.float32)
    summed = lax.psum_scatter(
        jnp.stack([blocks[:, 0, 0] + blocks[:, 1, 1], blocks[:, 0, 1] - blocks[:, 1, 0]], 1).astype(
            jnp.bfloat16
        ),
        "tm",
        scatter_dimension=0,
        tiled=True,
    )
    chan_index = lax.axis_index("chan")
    tm_index = lax.axis_index("tm")
    first_channel = chan_index * channel_count
    local_flags = lax.dynamic_slice_in_dim(channel_flags, first_channel, channel_count, 0)
    spectrum, baseline_stats = spectrum_terms(
        summed, first_channel, local_flags.astype(jnp.float32)
    )
    block_pairs = spectrum.shape[0]
    total_time = voltages.shape[0] * tm_size
    norm_factor = 1.0 / math.sqrt(CHANNELS * total_time)
    spectrum = lax.psum_scatter(spectrum, "chan", scatter_dimension=0, tiled=True)
    own_pairs = spectrum.shape[0]
    rm_spectrum = (spectrum * norm_factor).reshape(1, own_pairs, window, 2, DEPTH)
    all_stats = lax.dynamic_update_slice_in_dim(
        jnp.zeros((stations, window, 8), jnp.float32),
        baseline_stats,
        tm_index * block_pairs,
        0,
    )
    all_stats = lax.psum(all_stats, ("chan", "tm")) / CHANNELS
    station_axis = jnp.arange(stations, dtype=jnp.int32)
    window_map = (window_stations[:, None] == station_axis[None, :]).astype(jnp.float32)
    station_map = jnp.eye(stations, dtype=jnp.float32)
    leak_real = jnp.zeros((stations,), jnp.float32)
    leak_imag = jnp.zeros((stations,), jnp.float32)
    fields = [all_stats[:, :, column] for column in range(8)]
    for iteration in range(ITERATIONS):
        numer_real, numer_imag, weight_sum = station_terms(
            leak_real, leak_imag, fields, station_map, window_map
        )
        leak_real = numer_real / (weight_sum + 1e-06)
        leak_imag = numer_imag / (weight_sum + 1e-06)
    return (rm_spectrum, jnp.stack([leak_real, leak_imag], 0))


def solution(mesh):
    return jax.shard_map(
        per_device,
        mesh=mesh,
        in_specs=(P("tm", "chan", None, None), P(), P()),
        out_specs=(P("tm", "chan", None, None, None), P()),
        check_vma=False,
    )
```

```python
import math

import jax
import jax.numpy as jnp
from jax import lax
from jax.sharding import PartitionSpec as P

CHANNELS = 8192
DEPTH = 1024
ITERATIONS = 3


def phase_table(first_channel, channel_count):
    chan_pos = (first_channel + jnp.arange(channel_count, dtype=jnp.int32)).astype(jnp.float32)
    frequency = 1.0 + (chan_pos + 0.5) / CHANNELS
    lambda_sq = 1.0 / (frequency * frequency)
    depth_grid = (jnp.arange(DEPTH).astype(jnp.float32) - DEPTH // 2) * 2.0
    angles = 2.0 * depth_grid[None, :] * (lambda_sq[:, None] - 0.5)
    return (jnp.cos(angles).astype(jnp.bfloat16), jnp.sin(angles).astype(jnp.bfloat16))


def station_terms(leak_real, leak_imag, fields, station_map, window_map):
    far_real = jnp.sum(station_map * leak_real[None, :], 1)[:, None]
    far_imag = jnp.sum(station_map * leak_imag[None, :], 1)[:, None]
    near_real = jnp.sum(window_map * leak_real[None, :], 1)[None, :]
    near_imag = jnp.sum(window_map * leak_imag[None, :], 1)[None, :]
    row_real = fields[0] - (far_real * fields[2] + far_imag * fields[3])
    row_imag = fields[1] - (far_real * fields[3] - far_imag * fields[2])
    col_real = fields[4] - (near_real * fields[2] + near_imag * fields[3])
    col_imag = -(fields[5] - (near_imag * fields[2] - near_real * fields[3]))
    numer_real = jnp.sum(window_map * jnp.sum(row_real, 0)[:, None], 0) + jnp.sum(
        station_map * jnp.sum(col_real, 1)[:, None], 0
    )
    numer_imag = jnp.sum(window_map * jnp.sum(row_imag, 0)[:, None], 0) + jnp.sum(
        station_map * jnp.sum(col_imag, 1)[:, None], 0
    )
    weight_sum = jnp.sum(window_map * jnp.sum(fields[6], 0)[:, None], 0) + jnp.sum(
        station_map * jnp.sum(fields[7], 1)[:, None], 0
    )
    return (numer_real, numer_imag, weight_sum)


def spectrum_terms(local_vis, first_channel, flag_weights):
    pairs = local_vis.shape[0] // 2
    window = local_vis.shape[2] // 2
    channel_count = local_vis.shape[3]
    six = local_vis.reshape(pairs, 2, 2, window, 2, channel_count)

    def correlation(feed_a, feed_b):
        return six[:, feed_b, :, :, feed_a, :].astype(jnp.float32)

    corr_xx = correlation(0, 0)
    corr_xy = correlation(0, 1)
    corr_yx = correlation(1, 0)
    corr_yy = correlation(1, 1)
    pol_real = 0.5 * (corr_xx[:, 0] - corr_yy[:, 0]) - 0.5 * (corr_xy[:, 1] + corr_yx[:, 1])
    pol_imag = 0.5 * (corr_xx[:, 1] - corr_yy[:, 1]) + 0.5 * (corr_xy[:, 0] + corr_yx[:, 0])
    pol_real = (pol_real * flag_weights).astype(jnp.bfloat16).reshape(pairs * window, channel_count)
    pol_imag = (pol_imag * flag_weights).astype(jnp.bfloat16).reshape(pairs * window, channel_count)

    def conj_sum(left, right):
        real_part = jnp.sum(
            flag_weights * (left[:, 0] * right[:, 0] + left[:, 1] * right[:, 1]), -1
        )
        imag_part = jnp.sum(
            flag_weights * (left[:, 1] * right[:, 0] - left[:, 0] * right[:, 1]), -1
        )
        return (real_part, imag_part)

    cross_real, cross_imag = conj_sum(corr_xy, corr_yy)
    mixed_real, mixed_imag = conj_sum(corr_xx, corr_yy)
    side_real, side_imag = conj_sum(corr_xy, corr_xx)
    power_y = jnp.sum(
        flag_weights * (corr_yy[:, 0] * corr_yy[:, 0] + corr_yy[:, 1] * corr_yy[:, 1]), -1
    )
    power_x = jnp.sum(
        flag_weights * (corr_xx[:, 0] * corr_xx[:, 0] + corr_xx[:, 1] * corr_xx[:, 1]), -1
    )
    baseline_stats = jnp.stack(
        [cross_real, cross_imag, mixed_real, mixed_imag, side_real, side_imag, power_y, power_x], -1
    )
    block_width = math.gcd(channel_count, 1024)

    def add_block(block_id, total):
        offset = block_id * block_width
        cosine, sine_part = phase_table(first_channel + offset, block_width)
        left = jnp.concatenate(
            [
                lax.dynamic_slice_in_dim(pol_real, offset, block_width, 1),
                lax.dynamic_slice_in_dim(pol_imag, offset, block_width, 1),
            ],
            1,
        )
        right = jnp.concatenate(
            [jnp.concatenate([cosine, -sine_part], 1), jnp.concatenate([sine_part, cosine], 1)], 0
        )
        return total + jnp.dot(left, right, preferred_element_type=jnp.float32)

    total = lax.fori_loop(
        0,
        channel_count // block_width,
        add_block,
        jnp.zeros((pairs * window, 2 * DEPTH), jnp.float32),
    )
    return (total.reshape(pairs, window, 2 * DEPTH), baseline_stats)


def per_device(voltages, window_stations, channel_flags):
    tm_size = lax.axis_size("tm")
    chan_size = lax.axis_size("chan")
    inputs = voltages.shape[3]
    stations = inputs // 2
    window = window_stations.shape[0]
    channel_count = voltages.shape[1]
    feed_index = (2 * window_stations[:, None] + jnp.arange(2, dtype=jnp.int32)[None, :]).reshape(
        -1
    )
    picked = jnp.take(voltages, feed_index, axis=3)
    blocks = jnp.einsum("tcaw,tcbx->xbawc", picked, voltages, preferred_element_type=jnp.float32)
    partial = jnp.stack(
        [blocks[:, 0, 0] + blocks[:, 1, 1], blocks[:, 0, 1] - blocks[:, 1, 0]], 1
    ).astype(jnp.bfloat16)
    partial_shape = partial.shape
    summed = lax.psum_scatter(
        partial.reshape(partial_shape[0], -1, partial_shape[-1]),
        "tm",
        scatter_dimension=0,
        tiled=True,
    ).reshape(-1, *partial_shape[1:])
    chan_index = lax.axis_index("chan")
    tm_index = lax.axis_index("tm")
    first_channel = chan_index * channel_count
    local_flags = lax.dynamic_slice_in_dim(channel_flags, first_channel, channel_count, 0)
    spectrum, baseline_stats = spectrum_terms(
        summed, first_channel, local_flags.astype(jnp.float32)
    )
    block_pairs = spectrum.shape[0]
    total_time = voltages.shape[0] * tm_size
    norm_factor = 1.0 / math.sqrt(CHANNELS * total_time)
    spectrum = lax.psum_scatter(
        spectrum.reshape(block_pairs // 2, -1, DEPTH), "chan", scatter_dimension=0, tiled=True
    )
    own_pairs = block_pairs // chan_size
    rm_spectrum = (spectrum * norm_factor).reshape(1, own_pairs, window, 2, DEPTH)
    all_stats = lax.dynamic_update_slice_in_dim(
        jnp.zeros((stations, window, 8), jnp.float32),
        baseline_stats,
        tm_index * block_pairs,
        0,
    )
    all_stats = lax.psum(all_stats.reshape(-1, 128), ("chan", "tm")).reshape(all_stats.shape) / CHANNELS
    station_axis = jnp.arange(stations, dtype=jnp.int32)
    window_map = (window_stations[:, None] == station_axis[None, :]).astype(jnp.float32)
    station_map = jnp.eye(stations, dtype=jnp.float32)
    leak_real = jnp.zeros((stations,), jnp.float32)
    leak_imag = jnp.zeros((stations,), jnp.float32)
    fields = [all_stats[:, :, column] for column in range(8)]
    for iteration in range(ITERATIONS):
        numer_real, numer_imag, weight_sum = station_terms(
            leak_real, leak_imag, fields, station_map, window_map
        )
        leak_real = numer_real / (weight_sum + 1e-06)
        leak_imag = numer_imag / (weight_sum + 1e-06)
    return (rm_spectrum, jnp.stack([leak_real, leak_imag], 0))


def solution(mesh):
    return jax.shard_map(
        per_device,
        mesh=mesh,
        in_specs=(P("tm", "chan", None, None), P(), P()),
        out_specs=(P("tm", "chan", None, None, None), P()),
        check_vma=False,
    )
```

```python
import math

import jax
import jax.numpy as jnp
from jax import lax
from jax.sharding import PartitionSpec as P

CHANNELS = 8192
DEPTH = 1024
ITERATIONS = 3


def phase_table(first_channel, channel_count):
    chan_pos = (first_channel + jnp.arange(channel_count, dtype=jnp.int32)).astype(jnp.float32)
    frequency = 1.0 + (chan_pos + 0.5) / CHANNELS
    lambda_sq = 1.0 / (frequency * frequency)
    depth_grid = (jnp.arange(DEPTH).astype(jnp.float32) - DEPTH // 2) * 2.0
    angles = 2.0 * depth_grid[None, :] * (lambda_sq[:, None] - 0.5)
    return (jnp.cos(angles).astype(jnp.bfloat16), jnp.sin(angles).astype(jnp.bfloat16))


def station_terms(leak_real, leak_imag, fields, station_map, window_map):
    far_real = jnp.sum(station_map * leak_real[None, :], 1)[:, None]
    far_imag = jnp.sum(station_map * leak_imag[None, :], 1)[:, None]
    near_real = jnp.sum(window_map * leak_real[None, :], 1)[None, :]
    near_imag = jnp.sum(window_map * leak_imag[None, :], 1)[None, :]
    row_real = fields[0] - (far_real * fields[2] + far_imag * fields[3])
    row_imag = fields[1] - (far_real * fields[3] - far_imag * fields[2])
    col_real = fields[4] - (near_real * fields[2] + near_imag * fields[3])
    col_imag = -(fields[5] - (near_imag * fields[2] - near_real * fields[3]))
    numer_real = jnp.sum(window_map * jnp.sum(row_real, 0)[:, None], 0) + jnp.sum(
        station_map * jnp.sum(col_real, 1)[:, None], 0
    )
    numer_imag = jnp.sum(window_map * jnp.sum(row_imag, 0)[:, None], 0) + jnp.sum(
        station_map * jnp.sum(col_imag, 1)[:, None], 0
    )
    weight_sum = jnp.sum(window_map * jnp.sum(fields[6], 0)[:, None], 0) + jnp.sum(
        station_map * jnp.sum(fields[7], 1)[:, None], 0
    )
    return (numer_real, numer_imag, weight_sum)


def spectrum_terms(local_vis, first_channel, flag_weights):
    pairs = local_vis.shape[0] // 2
    window = local_vis.shape[2] // 2
    channel_count = local_vis.shape[3]
    six = local_vis.reshape(pairs, 2, 2, window, 2, channel_count)

    def correlation(feed_a, feed_b):
        return six[:, feed_b, :, :, feed_a, :].astype(jnp.float32)

    corr_xx = correlation(0, 0)
    corr_xy = correlation(0, 1)
    corr_yx = correlation(1, 0)
    corr_yy = correlation(1, 1)
    pol_real = 0.5 * (corr_xx[:, 0] - corr_yy[:, 0]) - 0.5 * (corr_xy[:, 1] + corr_yx[:, 1])
    pol_imag = 0.5 * (corr_xx[:, 1] - corr_yy[:, 1]) + 0.5 * (corr_xy[:, 0] + corr_yx[:, 0])
    pol_real = (pol_real * flag_weights).astype(jnp.bfloat16).reshape(pairs * window, channel_count)
    pol_imag = (pol_imag * flag_weights).astype(jnp.bfloat16).reshape(pairs * window, channel_count)

    def conj_sum(left, right):
        real_part = jnp.sum(
            flag_weights * (left[:, 0] * right[:, 0] + left[:, 1] * right[:, 1]), -1
        )
        imag_part = jnp.sum(
            flag_weights * (left[:, 1] * right[:, 0] - left[:, 0] * right[:, 1]), -1
        )
        return (real_part, imag_part)

    cross_real, cross_imag = conj_sum(corr_xy, corr_yy)
    mixed_real, mixed_imag = conj_sum(corr_xx, corr_yy)
    side_real, side_imag = conj_sum(corr_xy, corr_xx)
    power_y = jnp.sum(
        flag_weights * (corr_yy[:, 0] * corr_yy[:, 0] + corr_yy[:, 1] * corr_yy[:, 1]), -1
    )
    power_x = jnp.sum(
        flag_weights * (corr_xx[:, 0] * corr_xx[:, 0] + corr_xx[:, 1] * corr_xx[:, 1]), -1
    )
    baseline_stats = jnp.stack(
        [cross_real, cross_imag, mixed_real, mixed_imag, side_real, side_imag, power_y, power_x], -1
    )
    block_width = math.gcd(channel_count, 1024)

    def add_block(block_id, total):
        offset = block_id * block_width
        cosine, sine_part = phase_table(first_channel + offset, block_width)
        left = jnp.concatenate(
            [
                lax.dynamic_slice_in_dim(pol_real, offset, block_width, 1),
                lax.dynamic_slice_in_dim(pol_imag, offset, block_width, 1),
            ],
            1,
        )
        right = jnp.concatenate(
            [jnp.concatenate([cosine, -sine_part], 1), jnp.concatenate([sine_part, cosine], 1)], 0
        )
        return total + jnp.dot(left, right, preferred_element_type=jnp.float32)

    total = lax.fori_loop(
        0,
        channel_count // block_width,
        add_block,
        jnp.zeros((pairs * window, 2 * DEPTH), jnp.float32),
    )
    return (total.reshape(pairs, window, 2 * DEPTH), baseline_stats)


def per_device(voltages, window_stations, channel_flags):
    tm_size = lax.axis_size("tm")
    chan_size = lax.axis_size("chan")
    inputs = voltages.shape[3]
    stations = inputs // 2
    window = window_stations.shape[0]
    channel_count = voltages.shape[1]
    feed_index = (2 * window_stations[:, None] + jnp.arange(2, dtype=jnp.int32)[None, :]).reshape(
        -1
    )
    picked = jnp.take(voltages, feed_index, axis=3)
    blocks = jnp.einsum("tcaw,tcbx->xbawc", picked, voltages, preferred_element_type=jnp.float32)
    partial = jnp.stack(
        [blocks[:, 0, 0] + blocks[:, 1, 1], blocks[:, 0, 1] - blocks[:, 1, 0]], 1
    ).astype(jnp.bfloat16)
    partial_shape = partial.shape
    summed = lax.psum_scatter(
        partial.reshape(partial_shape[0], -1, partial_shape[-1]),
        "tm",
        scatter_dimension=0,
        tiled=True,
    ).reshape(-1, *partial_shape[1:])
    chan_index = lax.axis_index("chan")
    tm_index = lax.axis_index("tm")
    first_channel = chan_index * channel_count
    local_flags = lax.dynamic_slice_in_dim(channel_flags, first_channel, channel_count, 0)
    spectrum, baseline_stats = spectrum_terms(
        summed, first_channel, local_flags.astype(jnp.float32)
    )
    block_pairs = spectrum.shape[0]
    total_time = voltages.shape[0] * tm_size
    norm_factor = 1.0 / math.sqrt(CHANNELS * total_time)
    spectrum = lax.psum_scatter(
        spectrum.reshape(block_pairs // 2, -1, DEPTH), "chan", scatter_dimension=0, tiled=True
    )
    own_pairs = block_pairs // chan_size
    rm_spectrum = (spectrum * norm_factor).reshape(1, own_pairs, window, 2, DEPTH)
    all_stats = lax.all_gather(
        lax.psum(baseline_stats, "chan"), "tm", axis=0, tiled=True
    ) / CHANNELS
    station_axis = jnp.arange(stations, dtype=jnp.int32)
    window_map = (window_stations[:, None] == station_axis[None, :]).astype(jnp.float32)
    station_map = jnp.eye(stations, dtype=jnp.float32)
    leak_real = jnp.zeros((stations,), jnp.float32)
    leak_imag = jnp.zeros((stations,), jnp.float32)
    fields = [all_stats[:, :, column] for column in range(8)]
    for iteration in range(ITERATIONS):
        numer_real, numer_imag, weight_sum = station_terms(
            leak_real, leak_imag, fields, station_map, window_map
        )
        leak_real = numer_real / (weight_sum + 1e-06)
        leak_imag = numer_imag / (weight_sum + 1e-06)
    return (rm_spectrum, jnp.stack([leak_real, leak_imag], 0))


def solution(mesh):
    return jax.shard_map(
        per_device,
        mesh=mesh,
        in_specs=(P("tm", "chan", None, None), P(), P()),
        out_specs=(P("tm", "chan", None, None, None), P()),
        check_vma=False,
    )
```

```python
import math

import jax
import jax.numpy as jnp
from jax import lax
from jax.sharding import PartitionSpec as P

CHANNELS = 8192
DEPTH = 1024
ITERATIONS = 3


def phase_table(first_channel, channel_count):
    chan_pos = (first_channel + jnp.arange(channel_count, dtype=jnp.int32)).astype(jnp.float32)
    frequency = 1.0 + (chan_pos + 0.5) / CHANNELS
    lambda_sq = 1.0 / (frequency * frequency)
    depth_grid = (jnp.arange(DEPTH).astype(jnp.float32) - DEPTH // 2) * 2.0
    angles = 2.0 * depth_grid[None, :] * (lambda_sq[:, None] - 0.5)
    return (jnp.cos(angles).astype(jnp.bfloat16), jnp.sin(angles).astype(jnp.bfloat16))


def station_terms(leak_real, leak_imag, fields, station_map, window_map):
    far_real = jnp.sum(station_map * leak_real[None, :], 1)[:, None]
    far_imag = jnp.sum(station_map * leak_imag[None, :], 1)[:, None]
    near_real = jnp.sum(window_map * leak_real[None, :], 1)[None, :]
    near_imag = jnp.sum(window_map * leak_imag[None, :], 1)[None, :]
    row_real = fields[0] - (far_real * fields[2] + far_imag * fields[3])
    row_imag = fields[1] - (far_real * fields[3] - far_imag * fields[2])
    col_real = fields[4] - (near_real * fields[2] + near_imag * fields[3])
    col_imag = -(fields[5] - (near_imag * fields[2] - near_real * fields[3]))
    numer_real = jnp.sum(window_map * jnp.sum(row_real, 0)[:, None], 0) + jnp.sum(
        station_map * jnp.sum(col_real, 1)[:, None], 0
    )
    numer_imag = jnp.sum(window_map * jnp.sum(row_imag, 0)[:, None], 0) + jnp.sum(
        station_map * jnp.sum(col_imag, 1)[:, None], 0
    )
    weight_sum = jnp.sum(window_map * jnp.sum(fields[6], 0)[:, None], 0) + jnp.sum(
        station_map * jnp.sum(fields[7], 1)[:, None], 0
    )
    return (numer_real, numer_imag, weight_sum)


def spectrum_terms(local_vis, first_channel, flag_weights):
    pairs = local_vis.shape[0] // 2
    window = local_vis.shape[2] // 2
    channel_count = local_vis.shape[3]
    six = local_vis.reshape(pairs, 2, 2, window, 2, channel_count)

    def correlation(feed_a, feed_b):
        return six[:, feed_b, :, :, feed_a, :].astype(jnp.float32)

    corr_xx = correlation(0, 0)
    corr_xy = correlation(0, 1)
    corr_yx = correlation(1, 0)
    corr_yy = correlation(1, 1)
    pol_real = 0.5 * (corr_xx[:, 0] - corr_yy[:, 0]) - 0.5 * (corr_xy[:, 1] + corr_yx[:, 1])
    pol_imag = 0.5 * (corr_xx[:, 1] - corr_yy[:, 1]) + 0.5 * (corr_xy[:, 0] + corr_yx[:, 0])
    pol_real = (pol_real * flag_weights).astype(jnp.bfloat16).reshape(pairs * window, channel_count)
    pol_imag = (pol_imag * flag_weights).astype(jnp.bfloat16).reshape(pairs * window, channel_count)

    def conj_sum(left, right):
        real_part = jnp.sum(
            flag_weights * (left[:, 0] * right[:, 0] + left[:, 1] * right[:, 1]), -1
        )
        imag_part = jnp.sum(
            flag_weights * (left[:, 1] * right[:, 0] - left[:, 0] * right[:, 1]), -1
        )
        return (real_part, imag_part)

    cross_real, cross_imag = conj_sum(corr_xy, corr_yy)
    mixed_real, mixed_imag = conj_sum(corr_xx, corr_yy)
    side_real, side_imag = conj_sum(corr_xy, corr_xx)
    power_y = jnp.sum(
        flag_weights * (corr_yy[:, 0] * corr_yy[:, 0] + corr_yy[:, 1] * corr_yy[:, 1]), -1
    )
    power_x = jnp.sum(
        flag_weights * (corr_xx[:, 0] * corr_xx[:, 0] + corr_xx[:, 1] * corr_xx[:, 1]), -1
    )
    baseline_stats = jnp.stack(
        [cross_real, cross_imag, mixed_real, mixed_imag, side_real, side_imag, power_y, power_x], -1
    )
    block_width = math.gcd(channel_count, 1024)

    def add_block(block_id, total):
        offset = block_id * block_width
        cosine, sine_part = phase_table(first_channel + offset, block_width)
        left = jnp.concatenate(
            [
                lax.dynamic_slice_in_dim(pol_real, offset, block_width, 1),
                lax.dynamic_slice_in_dim(pol_imag, offset, block_width, 1),
            ],
            1,
        )
        right = jnp.concatenate(
            [jnp.concatenate([cosine, -sine_part], 1), jnp.concatenate([sine_part, cosine], 1)], 0
        )
        return total + jnp.dot(left, right, preferred_element_type=jnp.float32)

    total = lax.fori_loop(
        0,
        channel_count // block_width,
        add_block,
        jnp.zeros((pairs * window, 2 * DEPTH), jnp.float32),
    )
    return (total.reshape(pairs, window, 2 * DEPTH), baseline_stats)


def per_device(voltages, window_stations, channel_flags):
    tm_size = lax.axis_size("tm")
    chan_size = lax.axis_size("chan")
    inputs = voltages.shape[3]
    stations = inputs // 2
    window = window_stations.shape[0]
    channel_count = voltages.shape[1]
    feed_index = (2 * window_stations[:, None] + jnp.arange(2, dtype=jnp.int32)[None, :]).reshape(
        -1
    )
    picked = jnp.concatenate(
        [
            lax.dynamic_slice_in_dim(voltages, 2 * window_stations[k], 2, 3)
            for k in range(window)
        ],
        3,
    )
    left = jnp.stack(
        [picked, jnp.stack([picked[:, :, 1], -picked[:, :, 0]], 2)], 3
    )
    left = left.reshape(*picked.shape[:3], -1)
    partial = jnp.einsum(
        "tcrq,tcri->iqc", left, voltages, preferred_element_type=jnp.float32
    ).astype(jnp.bfloat16)
    partial_shape = (inputs, 2, 2 * window, channel_count)
    summed = lax.psum_scatter(
        partial,
        "tm",
        scatter_dimension=0,
        tiled=True,
    ).reshape(-1, *partial_shape[1:])
    chan_index = lax.axis_index("chan")
    tm_index = lax.axis_index("tm")
    first_channel = chan_index * channel_count
    local_flags = lax.dynamic_slice_in_dim(channel_flags, first_channel, channel_count, 0)
    spectrum, baseline_stats = spectrum_terms(
        summed, first_channel, local_flags.astype(jnp.float32)
    )
    block_pairs = spectrum.shape[0]
    total_time = voltages.shape[0] * tm_size
    norm_factor = 1.0 / math.sqrt(CHANNELS * total_time)
    spectrum = lax.psum_scatter(
        spectrum.reshape(block_pairs // 2, -1, DEPTH), "chan", scatter_dimension=0, tiled=True
    )
    own_pairs = block_pairs // chan_size
    rm_spectrum = (spectrum * norm_factor).reshape(1, own_pairs, window, 2, DEPTH)
    all_stats = lax.all_gather(
        lax.psum(baseline_stats, "chan"), "tm", axis=0, tiled=True
    ) / CHANNELS
    station_axis = jnp.arange(stations, dtype=jnp.int32)
    window_map = (window_stations[:, None] == station_axis[None, :]).astype(jnp.float32)
    station_map = jnp.eye(stations, dtype=jnp.float32)
    leak_real = jnp.zeros((stations,), jnp.float32)
    leak_imag = jnp.zeros((stations,), jnp.float32)
    fields = [all_stats[:, :, column] for column in range(8)]
    for iteration in range(ITERATIONS):
        numer_real, numer_imag, weight_sum = station_terms(
            leak_real, leak_imag, fields, station_map, window_map
        )
        leak_real = numer_real / (weight_sum + 1e-06)
        leak_imag = numer_imag / (weight_sum + 1e-06)
    return (rm_spectrum, jnp.stack([leak_real, leak_imag], 0))


def solution(mesh):
    return jax.shard_map(
        per_device,
        mesh=mesh,
        in_specs=(P("tm", "chan", None, None), P(), P()),
        out_specs=(P("tm", "chan", None, None, None), P()),
        check_vma=False,
    )
```

```python
import math

import jax
import jax.numpy as jnp
from jax import lax
from jax.sharding import PartitionSpec as P

CHANNELS = 8192
DEPTH = 1024
ITERATIONS = 3


def phase_table(first_channel, channel_count):
    chan_pos = (first_channel + jnp.arange(channel_count, dtype=jnp.int32)).astype(jnp.float32)
    frequency = 1.0 + (chan_pos + 0.5) / CHANNELS
    lambda_sq = 1.0 / (frequency * frequency)
    depth_grid = (jnp.arange(DEPTH).astype(jnp.float32) - DEPTH // 2) * 2.0
    angles = 2.0 * depth_grid[None, :] * (lambda_sq[:, None] - 0.5)
    return (jnp.cos(angles).astype(jnp.bfloat16), jnp.sin(angles).astype(jnp.bfloat16))


def station_terms(leak_real, leak_imag, fields, station_map, window_map):
    far_real = jnp.sum(station_map * leak_real[None, :], 1)[:, None]
    far_imag = jnp.sum(station_map * leak_imag[None, :], 1)[:, None]
    near_real = jnp.sum(window_map * leak_real[None, :], 1)[None, :]
    near_imag = jnp.sum(window_map * leak_imag[None, :], 1)[None, :]
    row_real = fields[0] - (far_real * fields[2] + far_imag * fields[3])
    row_imag = fields[1] - (far_real * fields[3] - far_imag * fields[2])
    col_real = fields[4] - (near_real * fields[2] + near_imag * fields[3])
    col_imag = -(fields[5] - (near_imag * fields[2] - near_real * fields[3]))
    numer_real = jnp.sum(window_map * jnp.sum(row_real, 0)[:, None], 0) + jnp.sum(
        station_map * jnp.sum(col_real, 1)[:, None], 0
    )
    numer_imag = jnp.sum(window_map * jnp.sum(row_imag, 0)[:, None], 0) + jnp.sum(
        station_map * jnp.sum(col_imag, 1)[:, None], 0
    )
    weight_sum = jnp.sum(window_map * jnp.sum(fields[6], 0)[:, None], 0) + jnp.sum(
        station_map * jnp.sum(fields[7], 1)[:, None], 0
    )
    return (numer_real, numer_imag, weight_sum)


def spectrum_terms(local_vis, first_channel, flag_weights):
    pairs = local_vis.shape[0] // 2
    window = local_vis.shape[2] // 2
    channel_count = local_vis.shape[3]
    six = local_vis.reshape(pairs, 2, 2, window, 2, channel_count)

    def correlation(feed_a, feed_b):
        return six[:, feed_b, :, :, feed_a, :].astype(jnp.float32)

    corr_xx = correlation(0, 0)
    corr_xy = correlation(0, 1)
    corr_yx = correlation(1, 0)
    corr_yy = correlation(1, 1)
    pol_real = 0.5 * (corr_xx[:, 0] - corr_yy[:, 0]) - 0.5 * (corr_xy[:, 1] + corr_yx[:, 1])
    pol_imag = 0.5 * (corr_xx[:, 1] - corr_yy[:, 1]) + 0.5 * (corr_xy[:, 0] + corr_yx[:, 0])
    pol_real = (pol_real * flag_weights).astype(jnp.bfloat16).reshape(pairs * window, channel_count)
    pol_imag = (pol_imag * flag_weights).astype(jnp.bfloat16).reshape(pairs * window, channel_count)

    def conj_sum(left, right):
        real_part = jnp.sum(
            flag_weights * (left[:, 0] * right[:, 0] + left[:, 1] * right[:, 1]), -1
        )
        imag_part = jnp.sum(
            flag_weights * (left[:, 1] * right[:, 0] - left[:, 0] * right[:, 1]), -1
        )
        return (real_part, imag_part)

    cross_real, cross_imag = conj_sum(corr_xy, corr_yy)
    mixed_real, mixed_imag = conj_sum(corr_xx, corr_yy)
    side_real, side_imag = conj_sum(corr_xy, corr_xx)
    power_y = jnp.sum(
        flag_weights * (corr_yy[:, 0] * corr_yy[:, 0] + corr_yy[:, 1] * corr_yy[:, 1]), -1
    )
    power_x = jnp.sum(
        flag_weights * (corr_xx[:, 0] * corr_xx[:, 0] + corr_xx[:, 1] * corr_xx[:, 1]), -1
    )
    baseline_stats = jnp.stack(
        [cross_real, cross_imag, mixed_real, mixed_imag, side_real, side_imag, power_y, power_x], -1
    )
    block_width = math.gcd(channel_count, 1024)

    def add_block(block_id, total):
        offset = block_id * block_width
        cosine, sine_part = phase_table(first_channel + offset, block_width)
        left = jnp.concatenate(
            [
                lax.dynamic_slice_in_dim(pol_real, offset, block_width, 1),
                lax.dynamic_slice_in_dim(pol_imag, offset, block_width, 1),
            ],
            1,
        )
        right = jnp.concatenate(
            [jnp.concatenate([cosine, -sine_part], 1), jnp.concatenate([sine_part, cosine], 1)], 0
        )
        return total + jnp.dot(left, right, preferred_element_type=jnp.float32)

    total = lax.fori_loop(
        0,
        channel_count // block_width,
        add_block,
        jnp.zeros((pairs * window, 2 * DEPTH), jnp.float32),
    )
    return (total.reshape(pairs, window, 2 * DEPTH), baseline_stats)


def per_device(voltages, window_stations, channel_flags):
    tm_size = lax.axis_size("tm")
    chan_size = lax.axis_size("chan")
    inputs = voltages.shape[3]
    stations = inputs // 2
    window = window_stations.shape[0]
    channel_count = voltages.shape[1]
    feed_index = (2 * window_stations[:, None] + jnp.arange(2, dtype=jnp.int32)[None, :]).reshape(
        -1
    )
    selector = (
        jnp.arange(inputs, dtype=jnp.int32)[:, None] == feed_index[None, :]
    ).astype(voltages.dtype)
    picked = jnp.einsum(
        "tcri,iw->tcrw", voltages, selector, preferred_element_type=jnp.float32
    ).astype(voltages.dtype)
    left = jnp.stack(
        [picked, jnp.stack([picked[:, :, 1], -picked[:, :, 0]], 2)], 3
    )
    left = left.reshape(*picked.shape[:3], -1)
    partial = jnp.einsum(
        "tcrq,tcri->iqc", left, voltages, preferred_element_type=jnp.float32
    ).astype(jnp.bfloat16)
    partial_shape = (inputs, 2, 2 * window, channel_count)
    summed = lax.psum_scatter(
        partial,
        "tm",
        scatter_dimension=0,
        tiled=True,
    ).reshape(-1, *partial_shape[1:])
    chan_index = lax.axis_index("chan")
    tm_index = lax.axis_index("tm")
    first_channel = chan_index * channel_count
    local_flags = lax.dynamic_slice_in_dim(channel_flags, first_channel, channel_count, 0)
    spectrum, baseline_stats = spectrum_terms(
        summed, first_channel, local_flags.astype(jnp.float32)
    )
    block_pairs = spectrum.shape[0]
    total_time = voltages.shape[0] * tm_size
    norm_factor = 1.0 / math.sqrt(CHANNELS * total_time)
    spectrum = lax.psum_scatter(
        spectrum.reshape(block_pairs // 2, -1, DEPTH), "chan", scatter_dimension=0, tiled=True
    )
    own_pairs = block_pairs // chan_size
    rm_spectrum = (spectrum * norm_factor).reshape(1, own_pairs, window, 2, DEPTH)
    all_stats = lax.all_gather(
        lax.psum(baseline_stats, "chan"), "tm", axis=0, tiled=True
    ) / CHANNELS
    station_axis = jnp.arange(stations, dtype=jnp.int32)
    window_map = (window_stations[:, None] == station_axis[None, :]).astype(jnp.float32)
    station_map = jnp.eye(stations, dtype=jnp.float32)
    leak_real = jnp.zeros((stations,), jnp.float32)
    leak_imag = jnp.zeros((stations,), jnp.float32)
    fields = [all_stats[:, :, column] for column in range(8)]
    for iteration in range(ITERATIONS):
        numer_real, numer_imag, weight_sum = station_terms(
            leak_real, leak_imag, fields, station_map, window_map
        )
        leak_real = numer_real / (weight_sum + 1e-06)
        leak_imag = numer_imag / (weight_sum + 1e-06)
    return (rm_spectrum, jnp.stack([leak_real, leak_imag], 0))


def solution(mesh):
    return jax.shard_map(
        per_device,
        mesh=mesh,
        in_specs=(P("tm", "chan", None, None), P(), P()),
        out_specs=(P("tm", "chan", None, None, None), P()),
        check_vma=False,
    )
```

```python
import math

import jax
import jax.numpy as jnp
from jax import lax
from jax.sharding import PartitionSpec as P

CHANNELS = 8192
DEPTH = 1024
ITERATIONS = 3
TM_CHUNKS = 2


def phase_table(first_channel, channel_count):
    chan_pos = (first_channel + jnp.arange(channel_count, dtype=jnp.int32)).astype(jnp.float32)
    frequency = 1.0 + (chan_pos + 0.5) / CHANNELS
    lambda_sq = 1.0 / (frequency * frequency)
    depth_grid = (jnp.arange(DEPTH).astype(jnp.float32) - DEPTH // 2) * 2.0
    angles = 2.0 * depth_grid[None, :] * (lambda_sq[:, None] - 0.5)
    return (jnp.cos(angles).astype(jnp.bfloat16), jnp.sin(angles).astype(jnp.bfloat16))


def station_terms(leak_real, leak_imag, fields, station_map, window_map):
    far_real = jnp.sum(station_map * leak_real[None, :], 1)[:, None]
    far_imag = jnp.sum(station_map * leak_imag[None, :], 1)[:, None]
    near_real = jnp.sum(window_map * leak_real[None, :], 1)[None, :]
    near_imag = jnp.sum(window_map * leak_imag[None, :], 1)[None, :]
    row_real = fields[0] - (far_real * fields[2] + far_imag * fields[3])
    row_imag = fields[1] - (far_real * fields[3] - far_imag * fields[2])
    col_real = fields[4] - (near_real * fields[2] + near_imag * fields[3])
    col_imag = -(fields[5] - (near_imag * fields[2] - near_real * fields[3]))
    numer_real = jnp.sum(window_map * jnp.sum(row_real, 0)[:, None], 0) + jnp.sum(
        station_map * jnp.sum(col_real, 1)[:, None], 0
    )
    numer_imag = jnp.sum(window_map * jnp.sum(row_imag, 0)[:, None], 0) + jnp.sum(
        station_map * jnp.sum(col_imag, 1)[:, None], 0
    )
    weight_sum = jnp.sum(window_map * jnp.sum(fields[6], 0)[:, None], 0) + jnp.sum(
        station_map * jnp.sum(fields[7], 1)[:, None], 0
    )
    return (numer_real, numer_imag, weight_sum)


def spectrum_terms(local_vis, first_channel, flag_weights):
    pairs = local_vis.shape[0] // 2
    window = local_vis.shape[2] // 2
    channel_count = local_vis.shape[3]
    six = local_vis.reshape(pairs, 2, 2, window, 2, channel_count)

    def correlation(feed_a, feed_b):
        return six[:, feed_b, :, :, feed_a, :].astype(jnp.float32)

    corr_xx = correlation(0, 0)
    corr_xy = correlation(0, 1)
    corr_yx = correlation(1, 0)
    corr_yy = correlation(1, 1)
    pol_real = 0.5 * (corr_xx[:, 0] - corr_yy[:, 0]) - 0.5 * (corr_xy[:, 1] + corr_yx[:, 1])
    pol_imag = 0.5 * (corr_xx[:, 1] - corr_yy[:, 1]) + 0.5 * (corr_xy[:, 0] + corr_yx[:, 0])
    pol_real = (pol_real * flag_weights).astype(jnp.bfloat16).reshape(pairs * window, channel_count)
    pol_imag = (pol_imag * flag_weights).astype(jnp.bfloat16).reshape(pairs * window, channel_count)

    def conj_sum(left, right):
        real_part = jnp.sum(
            flag_weights * (left[:, 0] * right[:, 0] + left[:, 1] * right[:, 1]), -1
        )
        imag_part = jnp.sum(
            flag_weights * (left[:, 1] * right[:, 0] - left[:, 0] * right[:, 1]), -1
        )
        return (real_part, imag_part)

    cross_real, cross_imag = conj_sum(corr_xy, corr_yy)
    mixed_real, mixed_imag = conj_sum(corr_xx, corr_yy)
    side_real, side_imag = conj_sum(corr_xy, corr_xx)
    power_y = jnp.sum(
        flag_weights * (corr_yy[:, 0] * corr_yy[:, 0] + corr_yy[:, 1] * corr_yy[:, 1]), -1
    )
    power_x = jnp.sum(
        flag_weights * (corr_xx[:, 0] * corr_xx[:, 0] + corr_xx[:, 1] * corr_xx[:, 1]), -1
    )
    baseline_stats = jnp.stack(
        [cross_real, cross_imag, mixed_real, mixed_imag, side_real, side_imag, power_y, power_x], -1
    )
    block_width = math.gcd(channel_count, 1024)

    def add_block(block_id, total):
        offset = block_id * block_width
        cosine, sine_part = phase_table(first_channel + offset, block_width)
        left = jnp.concatenate(
            [
                lax.dynamic_slice_in_dim(pol_real, offset, block_width, 1),
                lax.dynamic_slice_in_dim(pol_imag, offset, block_width, 1),
            ],
            1,
        )
        right = jnp.concatenate(
            [jnp.concatenate([cosine, -sine_part], 1), jnp.concatenate([sine_part, cosine], 1)], 0
        )
        return total + jnp.dot(left, right, preferred_element_type=jnp.float32)

    total = lax.fori_loop(
        0,
        channel_count // block_width,
        add_block,
        jnp.zeros((pairs * window, 2 * DEPTH), jnp.float32),
    )
    return (total.reshape(pairs, window, 2 * DEPTH), baseline_stats)


def per_device(voltages, window_stations, channel_flags):
    tm_size = lax.axis_size("tm")
    chan_size = lax.axis_size("chan")
    inputs = voltages.shape[3]
    stations = inputs // 2
    window = window_stations.shape[0]
    channel_count = voltages.shape[1]
    feed_index = (2 * window_stations[:, None] + jnp.arange(2, dtype=jnp.int32)[None, :]).reshape(
        -1
    )
    selector = (
        jnp.arange(inputs, dtype=jnp.int32)[:, None] == feed_index[None, :]
    ).astype(voltages.dtype)
    chunk = channel_count // TM_CHUNKS
    pieces = []
    for part in range(TM_CHUNKS):
        block = voltages[:, part * chunk : (part + 1) * chunk]
        picked = jnp.einsum(
            "tcri,iw->tcrw", block, selector, preferred_element_type=jnp.float32
        ).astype(voltages.dtype)
        left = jnp.stack(
            [picked, jnp.stack([picked[:, :, 1], -picked[:, :, 0]], 2)], 3
        )
        left = left.reshape(*picked.shape[:3], -1)
        partial = jnp.einsum(
            "tcrq,tcri->iqc", left, block, preferred_element_type=jnp.float32
        ).astype(jnp.bfloat16)
        pieces.append(lax.psum_scatter(partial, "tm", scatter_dimension=0, tiled=True))
    summed = jnp.concatenate(pieces, 2).reshape(-1, 2, 2 * window, channel_count)
    chan_index = lax.axis_index("chan")
    tm_index = lax.axis_index("tm")
    first_channel = chan_index * channel_count
    local_flags = lax.dynamic_slice_in_dim(channel_flags, first_channel, channel_count, 0)
    spectrum, baseline_stats = spectrum_terms(
        summed, first_channel, local_flags.astype(jnp.float32)
    )
    block_pairs = spectrum.shape[0]
    total_time = voltages.shape[0] * tm_size
    norm_factor = 1.0 / math.sqrt(CHANNELS * total_time)
    spectrum = lax.psum_scatter(
        spectrum.reshape(block_pairs // 2, -1, DEPTH), "chan", scatter_dimension=0, tiled=True
    )
    own_pairs = block_pairs // chan_size
    rm_spectrum = (spectrum * norm_factor).reshape(1, own_pairs, window, 2, DEPTH)
    all_stats = lax.all_gather(
        lax.psum(baseline_stats, "chan"), "tm", axis=0, tiled=True
    ) / CHANNELS
    station_axis = jnp.arange(stations, dtype=jnp.int32)
    window_map = (window_stations[:, None] == station_axis[None, :]).astype(jnp.float32)
    station_map = jnp.eye(stations, dtype=jnp.float32)
    leak_real = jnp.zeros((stations,), jnp.float32)
    leak_imag = jnp.zeros((stations,), jnp.float32)
    fields = [all_stats[:, :, column] for column in range(8)]
    for iteration in range(ITERATIONS):
        numer_real, numer_imag, weight_sum = station_terms(
            leak_real, leak_imag, fields, station_map, window_map
        )
        leak_real = numer_real / (weight_sum + 1e-06)
        leak_imag = numer_imag / (weight_sum + 1e-06)
    return (rm_spectrum, jnp.stack([leak_real, leak_imag], 0))


def solution(mesh):
    return jax.shard_map(
        per_device,
        mesh=mesh,
        in_specs=(P("tm", "chan", None, None), P(), P()),
        out_specs=(P("tm", "chan", None, None, None), P()),
        check_vma=False,
    )
```

```python
import math

import jax
import jax.numpy as jnp
from jax import lax
from jax.sharding import Mesh, PartitionSpec as P

CHANNELS = 8192
DEPTH = 1024
ITERATIONS = 3


def phase_table(first_channel, channel_count):
    chan_pos = (first_channel + jnp.arange(channel_count, dtype=jnp.int32)).astype(jnp.float32)
    frequency = 1.0 + (chan_pos + 0.5) / CHANNELS
    lambda_sq = 1.0 / (frequency * frequency)
    depth_grid = (jnp.arange(DEPTH).astype(jnp.float32) - DEPTH // 2) * 2.0
    angles = 2.0 * depth_grid[None, :] * (lambda_sq[:, None] - 0.5)
    return (jnp.cos(angles).astype(jnp.bfloat16), jnp.sin(angles).astype(jnp.bfloat16))


def station_terms(leak_real, leak_imag, fields, station_map, window_map):
    far_real = jnp.sum(station_map * leak_real[None, :], 1)[:, None]
    far_imag = jnp.sum(station_map * leak_imag[None, :], 1)[:, None]
    near_real = jnp.sum(window_map * leak_real[None, :], 1)[None, :]
    near_imag = jnp.sum(window_map * leak_imag[None, :], 1)[None, :]
    row_real = fields[0] - (far_real * fields[2] + far_imag * fields[3])
    row_imag = fields[1] - (far_real * fields[3] - far_imag * fields[2])
    col_real = fields[4] - (near_real * fields[2] + near_imag * fields[3])
    col_imag = -(fields[5] - (near_imag * fields[2] - near_real * fields[3]))
    numer_real = jnp.sum(window_map * jnp.sum(row_real, 0)[:, None], 0) + jnp.sum(
        station_map * jnp.sum(col_real, 1)[:, None], 0
    )
    numer_imag = jnp.sum(window_map * jnp.sum(row_imag, 0)[:, None], 0) + jnp.sum(
        station_map * jnp.sum(col_imag, 1)[:, None], 0
    )
    weight_sum = jnp.sum(window_map * jnp.sum(fields[6], 0)[:, None], 0) + jnp.sum(
        station_map * jnp.sum(fields[7], 1)[:, None], 0
    )
    return (numer_real, numer_imag, weight_sum)


def spectrum_terms(local_vis, first_channel, flag_weights):
    pairs = local_vis.shape[0] // 2
    window = local_vis.shape[2] // 2
    channel_count = local_vis.shape[3]
    six = local_vis.reshape(pairs, 2, 2, window, 2, channel_count)

    def correlation(feed_a, feed_b):
        return six[:, feed_b, :, :, feed_a, :].astype(jnp.float32)

    corr_xx = correlation(0, 0)
    corr_xy = correlation(0, 1)
    corr_yx = correlation(1, 0)
    corr_yy = correlation(1, 1)
    pol_real = 0.5 * (corr_xx[:, 0] - corr_yy[:, 0]) - 0.5 * (corr_xy[:, 1] + corr_yx[:, 1])
    pol_imag = 0.5 * (corr_xx[:, 1] - corr_yy[:, 1]) + 0.5 * (corr_xy[:, 0] + corr_yx[:, 0])
    pol_real = (pol_real * flag_weights).astype(jnp.bfloat16).reshape(pairs * window, channel_count)
    pol_imag = (pol_imag * flag_weights).astype(jnp.bfloat16).reshape(pairs * window, channel_count)

    def conj_sum(left, right):
        real_part = jnp.sum(
            flag_weights * (left[:, 0] * right[:, 0] + left[:, 1] * right[:, 1]), -1
        )
        imag_part = jnp.sum(
            flag_weights * (left[:, 1] * right[:, 0] - left[:, 0] * right[:, 1]), -1
        )
        return (real_part, imag_part)

    cross_real, cross_imag = conj_sum(corr_xy, corr_yy)
    mixed_real, mixed_imag = conj_sum(corr_xx, corr_yy)
    side_real, side_imag = conj_sum(corr_xy, corr_xx)
    power_y = jnp.sum(
        flag_weights * (corr_yy[:, 0] * corr_yy[:, 0] + corr_yy[:, 1] * corr_yy[:, 1]), -1
    )
    power_x = jnp.sum(
        flag_weights * (corr_xx[:, 0] * corr_xx[:, 0] + corr_xx[:, 1] * corr_xx[:, 1]), -1
    )
    baseline_stats = jnp.stack(
        [cross_real, cross_imag, mixed_real, mixed_imag, side_real, side_imag, power_y, power_x], -1
    )
    block_width = math.gcd(channel_count, 1024)

    def add_block(block_id, total):
        offset = block_id * block_width
        cosine, sine_part = phase_table(first_channel + offset, block_width)
        left = jnp.concatenate(
            [
                lax.dynamic_slice_in_dim(pol_real, offset, block_width, 1),
                lax.dynamic_slice_in_dim(pol_imag, offset, block_width, 1),
            ],
            1,
        )
        right = jnp.concatenate(
            [jnp.concatenate([cosine, -sine_part], 1), jnp.concatenate([sine_part, cosine], 1)], 0
        )
        return total + jnp.dot(left, right, preferred_element_type=jnp.float32)

    total = lax.fori_loop(
        0,
        channel_count // block_width,
        add_block,
        jnp.zeros((pairs * window, 2 * DEPTH), jnp.float32),
    )
    return (total.reshape(pairs, window, 2 * DEPTH), baseline_stats)


def per_device(voltages, window_stations, channel_flags):
    tm_size = lax.axis_size(("tm_major", "tm_minor"))
    chan_size = lax.axis_size("chan")
    inputs = voltages.shape[3]
    stations = inputs // 2
    window = window_stations.shape[0]
    channel_count = voltages.shape[1]
    feed_index = (2 * window_stations[:, None] + jnp.arange(2, dtype=jnp.int32)[None, :]).reshape(
        -1
    )
    selector = (
        jnp.arange(inputs, dtype=jnp.int32)[:, None] == feed_index[None, :]
    ).astype(voltages.dtype)
    picked = jnp.einsum(
        "tcri,iw->tcrw", voltages, selector, preferred_element_type=jnp.float32
    ).astype(voltages.dtype)
    left = jnp.stack(
        [picked, jnp.stack([picked[:, :, 1], -picked[:, :, 0]], 2)], 3
    )
    left = left.reshape(*picked.shape[:3], -1)
    partial = jnp.einsum(
        "tcrq,tcri->iqc", left, voltages, preferred_element_type=jnp.float32
    ).astype(jnp.bfloat16)
    partial_shape = (inputs, 2, 2 * window, channel_count)
    major = lax.axis_size("tm_major")
    minor = lax.axis_size("tm_minor")
    partial = partial.reshape(major, minor, -1, *partial.shape[1:])
    partial = jnp.swapaxes(partial, 0, 1).reshape(-1, *partial.shape[3:])
    summed = lax.psum_scatter(partial, "tm_minor", scatter_dimension=0, tiled=True)
    summed = lax.psum_scatter(summed, "tm_major", scatter_dimension=0, tiled=True)
    summed = summed.reshape(-1, *partial_shape[1:])
    chan_index = lax.axis_index("chan")
    tm_index = lax.axis_index(("tm_major", "tm_minor"))
    first_channel = chan_index * channel_count
    local_flags = lax.dynamic_slice_in_dim(channel_flags, first_channel, channel_count, 0)
    spectrum, baseline_stats = spectrum_terms(
        summed, first_channel, local_flags.astype(jnp.float32)
    )
    block_pairs = spectrum.shape[0]
    total_time = voltages.shape[0] * tm_size
    norm_factor = 1.0 / math.sqrt(CHANNELS * total_time)
    spectrum = lax.psum_scatter(
        spectrum.reshape(block_pairs // 2, -1, DEPTH), "chan", scatter_dimension=0, tiled=True
    )
    own_pairs = block_pairs // chan_size
    rm_spectrum = (spectrum * norm_factor).reshape(1, own_pairs, window, 2, DEPTH)
    all_stats = lax.all_gather(
        lax.psum(baseline_stats, "chan"), ("tm_major", "tm_minor"), axis=0, tiled=True
    ) / CHANNELS
    station_axis = jnp.arange(stations, dtype=jnp.int32)
    window_map = (window_stations[:, None] == station_axis[None, :]).astype(jnp.float32)
    station_map = jnp.eye(stations, dtype=jnp.float32)
    leak_real = jnp.zeros((stations,), jnp.float32)
    leak_imag = jnp.zeros((stations,), jnp.float32)
    fields = [all_stats[:, :, column] for column in range(8)]
    for iteration in range(ITERATIONS):
        numer_real, numer_imag, weight_sum = station_terms(
            leak_real, leak_imag, fields, station_map, window_map
        )
        leak_real = numer_real / (weight_sum + 1e-06)
        leak_imag = numer_imag / (weight_sum + 1e-06)
    return (rm_spectrum, jnp.stack([leak_real, leak_imag], 0))


def solution(mesh):
    chan_size, tm_size = mesh.devices.shape
    minor = math.isqrt(tm_size)
    if minor * minor != tm_size:
        minor = 1
    split_mesh = Mesh(
        mesh.devices.reshape(chan_size, tm_size // minor, minor),
        ("chan", "tm_major", "tm_minor"),
    )
    tm = ("tm_major", "tm_minor")
    return jax.shard_map(
        per_device,
        mesh=split_mesh,
        in_specs=(P(tm, "chan", None, None), P(), P()),
        out_specs=(P(tm, "chan", None, None, None), P()),
        check_vma=False,
    )
```

```python
import math

import jax
import jax.numpy as jnp
from jax import lax
from jax.sharding import PartitionSpec as P

CHANNELS = 8192
DEPTH = 1024
ITERATIONS = 3


def phase_table(first_channel, channel_count):
    chan_pos = (first_channel + jnp.arange(channel_count, dtype=jnp.int32)).astype(jnp.float32)
    frequency = 1.0 + (chan_pos + 0.5) / CHANNELS
    lambda_sq = 1.0 / (frequency * frequency)
    depth_grid = (jnp.arange(DEPTH).astype(jnp.float32) - DEPTH // 2) * 2.0
    angles = 2.0 * depth_grid[None, :] * (lambda_sq[:, None] - 0.5)
    return (jnp.cos(angles).astype(jnp.bfloat16), jnp.sin(angles).astype(jnp.bfloat16))


def station_terms(leak_real, leak_imag, fields, station_map, window_map):
    far_real = jnp.sum(station_map * leak_real[None, :], 1)[:, None]
    far_imag = jnp.sum(station_map * leak_imag[None, :], 1)[:, None]
    near_real = jnp.sum(window_map * leak_real[None, :], 1)[None, :]
    near_imag = jnp.sum(window_map * leak_imag[None, :], 1)[None, :]
    row_real = fields[0] - (far_real * fields[2] + far_imag * fields[3])
    row_imag = fields[1] - (far_real * fields[3] - far_imag * fields[2])
    col_real = fields[4] - (near_real * fields[2] + near_imag * fields[3])
    col_imag = -(fields[5] - (near_imag * fields[2] - near_real * fields[3]))
    numer_real = jnp.sum(window_map * jnp.sum(row_real, 0)[:, None], 0) + jnp.sum(
        station_map * jnp.sum(col_real, 1)[:, None], 0
    )
    numer_imag = jnp.sum(window_map * jnp.sum(row_imag, 0)[:, None], 0) + jnp.sum(
        station_map * jnp.sum(col_imag, 1)[:, None], 0
    )
    weight_sum = jnp.sum(window_map * jnp.sum(fields[6], 0)[:, None], 0) + jnp.sum(
        station_map * jnp.sum(fields[7], 1)[:, None], 0
    )
    return (numer_real, numer_imag, weight_sum)


def spectrum_terms(local_vis, first_channel, flag_weights):
    pairs = local_vis.shape[0] // 2
    window = local_vis.shape[2] // 2
    channel_count = local_vis.shape[3]
    six = local_vis.reshape(pairs, 2, 2, window, 2, channel_count)

    def correlation(feed_a, feed_b):
        return six[:, feed_b, :, :, feed_a, :].astype(jnp.float32)

    corr_xx = correlation(0, 0)
    corr_xy = correlation(0, 1)
    corr_yx = correlation(1, 0)
    corr_yy = correlation(1, 1)
    pol_real = 0.5 * (corr_xx[:, 0] - corr_yy[:, 0]) - 0.5 * (corr_xy[:, 1] + corr_yx[:, 1])
    pol_imag = 0.5 * (corr_xx[:, 1] - corr_yy[:, 1]) + 0.5 * (corr_xy[:, 0] + corr_yx[:, 0])
    pol_real = (pol_real * flag_weights).astype(jnp.bfloat16).reshape(pairs * window, channel_count)
    pol_imag = (pol_imag * flag_weights).astype(jnp.bfloat16).reshape(pairs * window, channel_count)

    def conj_sum(left, right):
        real_part = jnp.sum(
            flag_weights * (left[:, 0] * right[:, 0] + left[:, 1] * right[:, 1]), -1
        )
        imag_part = jnp.sum(
            flag_weights * (left[:, 1] * right[:, 0] - left[:, 0] * right[:, 1]), -1
        )
        return (real_part, imag_part)

    cross_real, cross_imag = conj_sum(corr_xy, corr_yy)
    mixed_real, mixed_imag = conj_sum(corr_xx, corr_yy)
    side_real, side_imag = conj_sum(corr_xy, corr_xx)
    power_y = jnp.sum(
        flag_weights * (corr_yy[:, 0] * corr_yy[:, 0] + corr_yy[:, 1] * corr_yy[:, 1]), -1
    )
    power_x = jnp.sum(
        flag_weights * (corr_xx[:, 0] * corr_xx[:, 0] + corr_xx[:, 1] * corr_xx[:, 1]), -1
    )
    baseline_stats = jnp.stack(
        [cross_real, cross_imag, mixed_real, mixed_imag, side_real, side_imag, power_y, power_x], -1
    )
    block_width = math.gcd(channel_count, 1024)

    def add_block(block_id, total):
        offset = block_id * block_width
        cosine, sine_part = phase_table(first_channel + offset, block_width)
        left = jnp.concatenate(
            [
                lax.dynamic_slice_in_dim(pol_real, offset, block_width, 1),
                lax.dynamic_slice_in_dim(pol_imag, offset, block_width, 1),
            ],
            1,
        )
        right = jnp.concatenate(
            [jnp.concatenate([cosine, -sine_part], 1), jnp.concatenate([sine_part, cosine], 1)], 0
        )
        return total + jnp.dot(left, right, preferred_element_type=jnp.float32)

    total = lax.fori_loop(
        0,
        channel_count // block_width,
        add_block,
        jnp.zeros((pairs * window, 2 * DEPTH), jnp.float32),
    )
    return (total.reshape(pairs, window, 2 * DEPTH), baseline_stats)


def per_device(voltages, window_stations, channel_flags):
    tm_size = lax.axis_size("tm")
    chan_size = lax.axis_size("chan")
    inputs = voltages.shape[3]
    stations = inputs // 2
    window = window_stations.shape[0]
    channel_count = voltages.shape[1]
    feed_index = (2 * window_stations[:, None] + jnp.arange(2, dtype=jnp.int32)[None, :]).reshape(
        -1
    )
    selector = (
        jnp.arange(inputs, dtype=jnp.int32)[:, None] == feed_index[None, :]
    ).astype(voltages.dtype)
    picked = jnp.einsum(
        "tcri,iw->tcrw", voltages, selector, preferred_element_type=jnp.float32
    ).astype(voltages.dtype)
    left = jnp.stack(
        [picked, jnp.stack([picked[:, :, 1], -picked[:, :, 0]], 2)], 3
    )
    left = left.reshape(*picked.shape[:3], -1)
    partial = jnp.einsum(
        "tcrq,tcri->iqc", left, voltages, preferred_element_type=jnp.float32
    ).astype(jnp.bfloat16)
    partial_shape = (inputs, 2, 2 * window, channel_count)
    summed = lax.psum_scatter(
        partial,
        "tm",
        scatter_dimension=0,
        tiled=True,
    ).reshape(-1, *partial_shape[1:])
    chan_index = lax.axis_index("chan")
    tm_index = lax.axis_index("tm")
    first_channel = chan_index * channel_count
    local_flags = lax.dynamic_slice_in_dim(channel_flags, first_channel, channel_count, 0)
    spectrum, baseline_stats = spectrum_terms(
        summed, first_channel, local_flags.astype(jnp.float32)
    )
    block_pairs = spectrum.shape[0]
    total_time = voltages.shape[0] * tm_size
    norm_factor = 1.0 / math.sqrt(CHANNELS * total_time)
    spectrum = lax.psum_scatter(
        spectrum.reshape(block_pairs // 2, -1, DEPTH), "chan", scatter_dimension=0, tiled=True
    )
    own_pairs = block_pairs // chan_size
    rm_spectrum = (spectrum * norm_factor).reshape(1, own_pairs, window, 2, DEPTH)
    chan_stats = lax.psum(baseline_stats, "chan").reshape(1, -1)
    padded = jnp.pad(chan_stats, ((0, 31), (0, (-chan_stats.shape[1]) % 128)))
    gathered = lax.all_gather(padded, "tm", axis=0, tiled=False)
    all_stats = gathered[:, 0, : chan_stats.shape[1]].reshape(
        stations, window, 8
    ) / CHANNELS
    station_axis = jnp.arange(stations, dtype=jnp.int32)
    window_map = (window_stations[:, None] == station_axis[None, :]).astype(jnp.float32)
    station_map = jnp.eye(stations, dtype=jnp.float32)
    leak_real = jnp.zeros((stations,), jnp.float32)
    leak_imag = jnp.zeros((stations,), jnp.float32)
    fields = [all_stats[:, :, column] for column in range(8)]
    for iteration in range(ITERATIONS):
        numer_real, numer_imag, weight_sum = station_terms(
            leak_real, leak_imag, fields, station_map, window_map
        )
        leak_real = numer_real / (weight_sum + 1e-06)
        leak_imag = numer_imag / (weight_sum + 1e-06)
    return (rm_spectrum, jnp.stack([leak_real, leak_imag], 0))


def solution(mesh):
    return jax.shard_map(
        per_device,
        mesh=mesh,
        in_specs=(P("tm", "chan", None, None), P(), P()),
        out_specs=(P("tm", "chan", None, None, None), P()),
        check_vma=False,
    )
```

```python
import math

import jax
import jax.numpy as jnp
from jax import lax
from jax.sharding import PartitionSpec as P

CHANNELS = 8192
DEPTH = 1024
ITERATIONS = 3


def phase_table(first_channel, channel_count):
    chan_pos = (first_channel + jnp.arange(channel_count, dtype=jnp.int32)).astype(jnp.float32)
    frequency = 1.0 + (chan_pos + 0.5) / CHANNELS
    lambda_sq = 1.0 / (frequency * frequency)
    depth_grid = (jnp.arange(DEPTH).astype(jnp.float32) - DEPTH // 2) * 2.0
    angles = 2.0 * depth_grid[None, :] * (lambda_sq[:, None] - 0.5)
    return (jnp.cos(angles).astype(jnp.bfloat16), jnp.sin(angles).astype(jnp.bfloat16))


def station_terms(leak_real, leak_imag, fields, station_map, window_map):
    far_real = jnp.sum(station_map * leak_real[None, :], 1)[:, None]
    far_imag = jnp.sum(station_map * leak_imag[None, :], 1)[:, None]
    near_real = jnp.sum(window_map * leak_real[None, :], 1)[None, :]
    near_imag = jnp.sum(window_map * leak_imag[None, :], 1)[None, :]
    row_real = fields[0] - (far_real * fields[2] + far_imag * fields[3])
    row_imag = fields[1] - (far_real * fields[3] - far_imag * fields[2])
    col_real = fields[4] - (near_real * fields[2] + near_imag * fields[3])
    col_imag = -(fields[5] - (near_imag * fields[2] - near_real * fields[3]))
    numer_real = jnp.sum(window_map * jnp.sum(row_real, 0)[:, None], 0) + jnp.sum(
        station_map * jnp.sum(col_real, 1)[:, None], 0
    )
    numer_imag = jnp.sum(window_map * jnp.sum(row_imag, 0)[:, None], 0) + jnp.sum(
        station_map * jnp.sum(col_imag, 1)[:, None], 0
    )
    weight_sum = jnp.sum(window_map * jnp.sum(fields[6], 0)[:, None], 0) + jnp.sum(
        station_map * jnp.sum(fields[7], 1)[:, None], 0
    )
    return (numer_real, numer_imag, weight_sum)


def spectrum_terms(local_vis, first_channel, flag_weights):
    pairs = local_vis.shape[0] // 2
    window = local_vis.shape[2] // 2
    channel_count = local_vis.shape[3]
    six = local_vis.reshape(pairs, 2, 2, window, 2, channel_count)

    def correlation(feed_a, feed_b):
        return six[:, feed_b, :, :, feed_a, :].astype(jnp.float32)

    corr_xx = correlation(0, 0)
    corr_xy = correlation(0, 1)
    corr_yx = correlation(1, 0)
    corr_yy = correlation(1, 1)
    pol_real = 0.5 * (corr_xx[:, 0] - corr_yy[:, 0]) - 0.5 * (corr_xy[:, 1] + corr_yx[:, 1])
    pol_imag = 0.5 * (corr_xx[:, 1] - corr_yy[:, 1]) + 0.5 * (corr_xy[:, 0] + corr_yx[:, 0])
    pol_real = (pol_real * flag_weights).astype(jnp.bfloat16).reshape(pairs * window, channel_count)
    pol_imag = (pol_imag * flag_weights).astype(jnp.bfloat16).reshape(pairs * window, channel_count)

    def conj_sum(left, right):
        real_part = jnp.sum(
            flag_weights * (left[:, 0] * right[:, 0] + left[:, 1] * right[:, 1]), -1
        )
        imag_part = jnp.sum(
            flag_weights * (left[:, 1] * right[:, 0] - left[:, 0] * right[:, 1]), -1
        )
        return (real_part, imag_part)

    cross_real, cross_imag = conj_sum(corr_xy, corr_yy)
    mixed_real, mixed_imag = conj_sum(corr_xx, corr_yy)
    side_real, side_imag = conj_sum(corr_xy, corr_xx)
    power_y = jnp.sum(
        flag_weights * (corr_yy[:, 0] * corr_yy[:, 0] + corr_yy[:, 1] * corr_yy[:, 1]), -1
    )
    power_x = jnp.sum(
        flag_weights * (corr_xx[:, 0] * corr_xx[:, 0] + corr_xx[:, 1] * corr_xx[:, 1]), -1
    )
    baseline_stats = jnp.stack(
        [cross_real, cross_imag, mixed_real, mixed_imag, side_real, side_imag, power_y, power_x], -1
    )
    block_width = math.gcd(channel_count, 1024)

    def add_block(block_id, total):
        offset = block_id * block_width
        cosine, sine_part = phase_table(first_channel + offset, block_width)
        left = jnp.concatenate(
            [
                lax.dynamic_slice_in_dim(pol_real, offset, block_width, 1),
                lax.dynamic_slice_in_dim(pol_imag, offset, block_width, 1),
            ],
            1,
        )
        right = jnp.concatenate(
            [jnp.concatenate([cosine, -sine_part], 1), jnp.concatenate([sine_part, cosine], 1)], 0
        )
        return total + jnp.dot(left, right, preferred_element_type=jnp.float32)

    total = lax.fori_loop(
        0,
        channel_count // block_width,
        add_block,
        jnp.zeros((pairs * window, 2 * DEPTH), jnp.float32),
    )
    return (total.reshape(pairs, window, 2 * DEPTH), baseline_stats)


def per_device(voltages, window_stations, channel_flags):
    tm_size = lax.axis_size("tm")
    chan_size = lax.axis_size("chan")
    inputs = voltages.shape[3]
    stations = inputs // 2
    window = window_stations.shape[0]
    channel_count = voltages.shape[1]
    feed_index = (2 * window_stations[:, None] + jnp.arange(2, dtype=jnp.int32)[None, :]).reshape(
        -1
    )
    selector = (
        jnp.arange(inputs, dtype=jnp.int32)[:, None] == feed_index[None, :]
    ).astype(voltages.dtype)
    picked = jnp.einsum(
        "tcri,iw->tcrw", voltages, selector, preferred_element_type=jnp.float32
    ).astype(voltages.dtype)
    left = jnp.stack(
        [picked, jnp.stack([picked[:, :, 1], -picked[:, :, 0]], 2)], 3
    )
    left = left.reshape(*picked.shape[:3], -1)
    partial = jnp.einsum(
        "tcrq,tcri->iqc", left, voltages, preferred_element_type=jnp.float32
    ).astype(jnp.bfloat16)
    partial_shape = (inputs, 2, 2 * window, channel_count)
    summed = lax.psum_scatter(
        partial,
        "tm",
        scatter_dimension=0,
        tiled=True,
    ).reshape(-1, *partial_shape[1:])
    chan_index = lax.axis_index("chan")
    tm_index = lax.axis_index("tm")
    first_channel = chan_index * channel_count
    local_flags = lax.dynamic_slice_in_dim(channel_flags, first_channel, channel_count, 0)
    spectrum, baseline_stats = spectrum_terms(
        summed, first_channel, local_flags.astype(jnp.float32)
    )
    block_pairs = spectrum.shape[0]
    total_time = voltages.shape[0] * tm_size
    norm_factor = 1.0 / math.sqrt(CHANNELS * total_time)
    spectrum = lax.psum_scatter(
        spectrum.reshape(block_pairs // 2, -1, DEPTH), "chan", scatter_dimension=0, tiled=True
    )
    own_pairs = block_pairs // chan_size
    rm_spectrum = (spectrum * norm_factor).reshape(1, own_pairs, window, 2, DEPTH)
    chan_stats = lax.psum(baseline_stats, "chan").reshape(1, -1)
    padded = jnp.pad(chan_stats, ((0, 63), (0, (-chan_stats.shape[1]) % 128)))
    gathered = lax.all_gather(padded, "tm", axis=0, tiled=False)
    all_stats = gathered[:, 0, : chan_stats.shape[1]].reshape(
        stations, window, 8
    ) / CHANNELS
    station_axis = jnp.arange(stations, dtype=jnp.int32)
    window_map = (window_stations[:, None] == station_axis[None, :]).astype(jnp.float32)
    station_map = jnp.eye(stations, dtype=jnp.float32)
    leak_real = jnp.zeros((stations,), jnp.float32)
    leak_imag = jnp.zeros((stations,), jnp.float32)
    fields = [all_stats[:, :, column] for column in range(8)]
    for iteration in range(ITERATIONS):
        numer_real, numer_imag, weight_sum = station_terms(
            leak_real, leak_imag, fields, station_map, window_map
        )
        leak_real = numer_real / (weight_sum + 1e-06)
        leak_imag = numer_imag / (weight_sum + 1e-06)
    return (rm_spectrum, jnp.stack([leak_real, leak_imag], 0))


def solution(mesh):
    return jax.shard_map(
        per_device,
        mesh=mesh,
        in_specs=(P("tm", "chan", None, None), P(), P()),
        out_specs=(P("tm", "chan", None, None, None), P()),
        check_vma=False,
    )
```

```python
import math

import jax
import jax.numpy as jnp
from jax import lax
from jax.sharding import PartitionSpec as P

CHANNELS = 8192
DEPTH = 1024
ITERATIONS = 3


def phase_table(first_channel, channel_count):
    chan_pos = (first_channel + jnp.arange(channel_count, dtype=jnp.int32)).astype(jnp.float32)
    frequency = 1.0 + (chan_pos + 0.5) / CHANNELS
    lambda_sq = 1.0 / (frequency * frequency)
    depth_grid = (jnp.arange(DEPTH).astype(jnp.float32) - DEPTH // 2) * 2.0
    angles = 2.0 * depth_grid[None, :] * (lambda_sq[:, None] - 0.5)
    return (jnp.cos(angles).astype(jnp.bfloat16), jnp.sin(angles).astype(jnp.bfloat16))


def station_terms(leak_real, leak_imag, fields, station_map, window_map):
    far_real = jnp.sum(station_map * leak_real[None, :], 1)[:, None]
    far_imag = jnp.sum(station_map * leak_imag[None, :], 1)[:, None]
    near_real = jnp.sum(window_map * leak_real[None, :], 1)[None, :]
    near_imag = jnp.sum(window_map * leak_imag[None, :], 1)[None, :]
    row_real = fields[0] - (far_real * fields[2] + far_imag * fields[3])
    row_imag = fields[1] - (far_real * fields[3] - far_imag * fields[2])
    col_real = fields[4] - (near_real * fields[2] + near_imag * fields[3])
    col_imag = -(fields[5] - (near_imag * fields[2] - near_real * fields[3]))
    numer_real = jnp.sum(window_map * jnp.sum(row_real, 0)[:, None], 0) + jnp.sum(
        station_map * jnp.sum(col_real, 1)[:, None], 0
    )
    numer_imag = jnp.sum(window_map * jnp.sum(row_imag, 0)[:, None], 0) + jnp.sum(
        station_map * jnp.sum(col_imag, 1)[:, None], 0
    )
    weight_sum = jnp.sum(window_map * jnp.sum(fields[6], 0)[:, None], 0) + jnp.sum(
        station_map * jnp.sum(fields[7], 1)[:, None], 0
    )
    return (numer_real, numer_imag, weight_sum)


def spectrum_terms(local_vis, first_channel, flag_weights):
    pairs = local_vis.shape[0] // 2
    window = local_vis.shape[2] // 2
    channel_count = local_vis.shape[3]
    six = local_vis.reshape(pairs, 2, 2, window, 2, channel_count)

    def correlation(feed_a, feed_b):
        return six[:, feed_b, :, :, feed_a, :].astype(jnp.float32)

    corr_xx = correlation(0, 0)
    corr_xy = correlation(0, 1)
    corr_yx = correlation(1, 0)
    corr_yy = correlation(1, 1)
    pol_real = 0.5 * (corr_xx[:, 0] - corr_yy[:, 0]) - 0.5 * (corr_xy[:, 1] + corr_yx[:, 1])
    pol_imag = 0.5 * (corr_xx[:, 1] - corr_yy[:, 1]) + 0.5 * (corr_xy[:, 0] + corr_yx[:, 0])
    pol_real = (pol_real * flag_weights).astype(jnp.bfloat16).reshape(pairs * window, channel_count)
    pol_imag = (pol_imag * flag_weights).astype(jnp.bfloat16).reshape(pairs * window, channel_count)

    def conj_sum(left, right):
        real_part = jnp.sum(
            flag_weights * (left[:, 0] * right[:, 0] + left[:, 1] * right[:, 1]), -1
        )
        imag_part = jnp.sum(
            flag_weights * (left[:, 1] * right[:, 0] - left[:, 0] * right[:, 1]), -1
        )
        return (real_part, imag_part)

    cross_real, cross_imag = conj_sum(corr_xy, corr_yy)
    mixed_real, mixed_imag = conj_sum(corr_xx, corr_yy)
    side_real, side_imag = conj_sum(corr_xy, corr_xx)
    power_y = jnp.sum(
        flag_weights * (corr_yy[:, 0] * corr_yy[:, 0] + corr_yy[:, 1] * corr_yy[:, 1]), -1
    )
    power_x = jnp.sum(
        flag_weights * (corr_xx[:, 0] * corr_xx[:, 0] + corr_xx[:, 1] * corr_xx[:, 1]), -1
    )
    baseline_stats = jnp.stack(
        [cross_real, cross_imag, mixed_real, mixed_imag, side_real, side_imag, power_y, power_x], -1
    )
    block_width = math.gcd(channel_count, 1024)

    def add_block(block_id, total):
        offset = block_id * block_width
        cosine, sine_part = phase_table(first_channel + offset, block_width)
        left = jnp.concatenate(
            [
                lax.dynamic_slice_in_dim(pol_real, offset, block_width, 1),
                lax.dynamic_slice_in_dim(pol_imag, offset, block_width, 1),
            ],
            1,
        )
        right = jnp.concatenate(
            [jnp.concatenate([cosine, -sine_part], 1), jnp.concatenate([sine_part, cosine], 1)], 0
        )
        return total + jnp.dot(left, right, preferred_element_type=jnp.float32)

    total = lax.fori_loop(
        0,
        channel_count // block_width,
        add_block,
        jnp.zeros((pairs * window, 2 * DEPTH), jnp.float32),
    )
    return (total.reshape(pairs, window, 2 * DEPTH), baseline_stats)


def butterfly_sum(value, axis):
    size = lax.axis_size(axis)
    distance = 1
    while distance < size:
        pairs = [(index, index ^ distance) for index in range(size)]
        value = value + lax.ppermute(value, axis, pairs)
        distance *= 2
    return value


def butterfly_gather(value, axis):
    size = lax.axis_size(axis)
    index = lax.axis_index(axis)
    distance = 1
    while distance < size:
        pairs = [(source, source ^ distance) for source in range(size)]
        other = lax.ppermute(value, axis, pairs)
        lower = (index & distance) == 0
        value = jnp.where(
            lower, jnp.concatenate([value, other], 0), jnp.concatenate([other, value], 0)
        )
        distance *= 2
    return value


def per_device(voltages, window_stations, channel_flags):
    tm_size = lax.axis_size("tm")
    chan_size = lax.axis_size("chan")
    inputs = voltages.shape[3]
    stations = inputs // 2
    window = window_stations.shape[0]
    channel_count = voltages.shape[1]
    feed_index = (2 * window_stations[:, None] + jnp.arange(2, dtype=jnp.int32)[None, :]).reshape(
        -1
    )
    selector = (
        jnp.arange(inputs, dtype=jnp.int32)[:, None] == feed_index[None, :]
    ).astype(voltages.dtype)
    picked = jnp.einsum(
        "tcri,iw->tcrw", voltages, selector, preferred_element_type=jnp.float32
    ).astype(voltages.dtype)
    left = jnp.stack(
        [picked, jnp.stack([picked[:, :, 1], -picked[:, :, 0]], 2)], 3
    )
    left = left.reshape(*picked.shape[:3], -1)
    partial = jnp.einsum(
        "tcrq,tcri->iqc", left, voltages, preferred_element_type=jnp.float32
    ).astype(jnp.bfloat16)
    partial_shape = (inputs, 2, 2 * window, channel_count)
    summed = lax.psum_scatter(
        partial,
        "tm",
        scatter_dimension=0,
        tiled=True,
    ).reshape(-1, *partial_shape[1:])
    chan_index = lax.axis_index("chan")
    tm_index = lax.axis_index("tm")
    first_channel = chan_index * channel_count
    local_flags = lax.dynamic_slice_in_dim(channel_flags, first_channel, channel_count, 0)
    spectrum, baseline_stats = spectrum_terms(
        summed, first_channel, local_flags.astype(jnp.float32)
    )
    block_pairs = spectrum.shape[0]
    total_time = voltages.shape[0] * tm_size
    norm_factor = 1.0 / math.sqrt(CHANNELS * total_time)
    spectrum = lax.psum_scatter(
        spectrum.reshape(block_pairs // 2, -1, DEPTH), "chan", scatter_dimension=0, tiled=True
    )
    own_pairs = block_pairs // chan_size
    rm_spectrum = (spectrum * norm_factor).reshape(1, own_pairs, window, 2, DEPTH)
    all_stats = butterfly_gather(butterfly_sum(baseline_stats, "chan"), "tm") / CHANNELS
    station_axis = jnp.arange(stations, dtype=jnp.int32)
    window_map = (window_stations[:, None] == station_axis[None, :]).astype(jnp.float32)
    station_map = jnp.eye(stations, dtype=jnp.float32)
    leak_real = jnp.zeros((stations,), jnp.float32)
    leak_imag = jnp.zeros((stations,), jnp.float32)
    fields = [all_stats[:, :, column] for column in range(8)]
    for iteration in range(ITERATIONS):
        numer_real, numer_imag, weight_sum = station_terms(
            leak_real, leak_imag, fields, station_map, window_map
        )
        leak_real = numer_real / (weight_sum + 1e-06)
        leak_imag = numer_imag / (weight_sum + 1e-06)
    return (rm_spectrum, jnp.stack([leak_real, leak_imag], 0))


def solution(mesh):
    return jax.shard_map(
        per_device,
        mesh=mesh,
        in_specs=(P("tm", "chan", None, None), P(), P()),
        out_specs=(P("tm", "chan", None, None, None), P()),
        check_vma=False,
    )
```

```python
import math

import jax
import jax.numpy as jnp
from jax import lax
from jax.sharding import PartitionSpec as P

CHANNELS = 8192
DEPTH = 1024
ITERATIONS = 3


def phase_table(first_channel, channel_count):
    chan_pos = (first_channel + jnp.arange(channel_count, dtype=jnp.int32)).astype(jnp.float32)
    frequency = 1.0 + (chan_pos + 0.5) / CHANNELS
    lambda_sq = 1.0 / (frequency * frequency)
    depth_grid = (jnp.arange(DEPTH).astype(jnp.float32) - DEPTH // 2) * 2.0
    angles = 2.0 * depth_grid[None, :] * (lambda_sq[:, None] - 0.5)
    return (jnp.cos(angles).astype(jnp.bfloat16), jnp.sin(angles).astype(jnp.bfloat16))


def station_terms(leak_real, leak_imag, fields, station_map, window_map):
    far_real = jnp.sum(station_map * leak_real[None, :], 1)[:, None]
    far_imag = jnp.sum(station_map * leak_imag[None, :], 1)[:, None]
    near_real = jnp.sum(window_map * leak_real[None, :], 1)[None, :]
    near_imag = jnp.sum(window_map * leak_imag[None, :], 1)[None, :]
    row_real = fields[0] - (far_real * fields[2] + far_imag * fields[3])
    row_imag = fields[1] - (far_real * fields[3] - far_imag * fields[2])
    col_real = fields[4] - (near_real * fields[2] + near_imag * fields[3])
    col_imag = -(fields[5] - (near_imag * fields[2] - near_real * fields[3]))
    numer_real = jnp.sum(window_map * jnp.sum(row_real, 0)[:, None], 0) + jnp.sum(
        station_map * jnp.sum(col_real, 1)[:, None], 0
    )
    numer_imag = jnp.sum(window_map * jnp.sum(row_imag, 0)[:, None], 0) + jnp.sum(
        station_map * jnp.sum(col_imag, 1)[:, None], 0
    )
    weight_sum = jnp.sum(window_map * jnp.sum(fields[6], 0)[:, None], 0) + jnp.sum(
        station_map * jnp.sum(fields[7], 1)[:, None], 0
    )
    return (numer_real, numer_imag, weight_sum)


def spectrum_terms(local_vis, first_channel, flag_weights):
    pairs = local_vis.shape[0] // 2
    window = local_vis.shape[2] // 2
    channel_count = local_vis.shape[3]
    six = local_vis.reshape(pairs, 2, 2, window, 2, channel_count)

    def correlation(feed_a, feed_b):
        return six[:, feed_b, :, :, feed_a, :].astype(jnp.float32)

    corr_xx = correlation(0, 0)
    corr_xy = correlation(0, 1)
    corr_yx = correlation(1, 0)
    corr_yy = correlation(1, 1)
    pol_real = 0.5 * (corr_xx[:, 0] - corr_yy[:, 0]) - 0.5 * (corr_xy[:, 1] + corr_yx[:, 1])
    pol_imag = 0.5 * (corr_xx[:, 1] - corr_yy[:, 1]) + 0.5 * (corr_xy[:, 0] + corr_yx[:, 0])
    pol_real = (pol_real * flag_weights).astype(jnp.bfloat16).reshape(pairs * window, channel_count)
    pol_imag = (pol_imag * flag_weights).astype(jnp.bfloat16).reshape(pairs * window, channel_count)

    def conj_sum(left, right):
        real_part = jnp.sum(
            flag_weights * (left[:, 0] * right[:, 0] + left[:, 1] * right[:, 1]), -1
        )
        imag_part = jnp.sum(
            flag_weights * (left[:, 1] * right[:, 0] - left[:, 0] * right[:, 1]), -1
        )
        return (real_part, imag_part)

    cross_real, cross_imag = conj_sum(corr_xy, corr_yy)
    mixed_real, mixed_imag = conj_sum(corr_xx, corr_yy)
    side_real, side_imag = conj_sum(corr_xy, corr_xx)
    power_y = jnp.sum(
        flag_weights * (corr_yy[:, 0] * corr_yy[:, 0] + corr_yy[:, 1] * corr_yy[:, 1]), -1
    )
    power_x = jnp.sum(
        flag_weights * (corr_xx[:, 0] * corr_xx[:, 0] + corr_xx[:, 1] * corr_xx[:, 1]), -1
    )
    baseline_stats = jnp.stack(
        [cross_real, cross_imag, mixed_real, mixed_imag, side_real, side_imag, power_y, power_x], -1
    )
    block_width = math.gcd(channel_count, 1024)

    def add_block(block_id, total):
        offset = block_id * block_width
        cosine, sine_part = phase_table(first_channel + offset, block_width)
        left = jnp.concatenate(
            [
                lax.dynamic_slice_in_dim(pol_real, offset, block_width, 1),
                lax.dynamic_slice_in_dim(pol_imag, offset, block_width, 1),
            ],
            1,
        )
        right = jnp.concatenate(
            [jnp.concatenate([cosine, -sine_part], 1), jnp.concatenate([sine_part, cosine], 1)], 0
        )
        return total + jnp.dot(left, right, preferred_element_type=jnp.float32)

    total = lax.fori_loop(
        0,
        channel_count // block_width,
        add_block,
        jnp.zeros((pairs * window, 2 * DEPTH), jnp.float32),
    )
    return (total.reshape(pairs, window, 2 * DEPTH), baseline_stats)


def per_device(voltages, window_stations, channel_flags):
    tm_size = lax.axis_size("tm")
    chan_size = lax.axis_size("chan")
    inputs = voltages.shape[3]
    stations = inputs // 2
    window = window_stations.shape[0]
    channel_count = voltages.shape[1]
    feed_index = (2 * window_stations[:, None] + jnp.arange(2, dtype=jnp.int32)[None, :]).reshape(
        -1
    )
    onehot = (
        jnp.arange(inputs, dtype=jnp.int32)[:, None] == feed_index[None, :]
    ).astype(jnp.float32)
    zero = jnp.zeros_like(onehot)
    selector = jnp.stack(
        [
            jnp.stack([jnp.stack([onehot, zero], 1), jnp.stack([zero, -onehot], 1)], 1),
            jnp.stack([jnp.stack([zero, onehot], 1), jnp.stack([onehot, zero], 1)], 1),
        ],
        0,
    ).reshape(2, inputs, 2, -1).astype(voltages.dtype)
    left = jnp.einsum(
        "tcsi,sirq->tcrq", voltages, selector, preferred_element_type=jnp.float32
    ).astype(voltages.dtype)
    partial = jnp.einsum(
        "tcrq,tcri->iqc", left, voltages, preferred_element_type=jnp.float32
    ).astype(jnp.bfloat16)
    partial_shape = (inputs, 2, 2 * window, channel_count)
    summed = lax.psum_scatter(
        partial,
        "tm",
        scatter_dimension=0,
        tiled=True,
    ).reshape(-1, *partial_shape[1:])
    chan_index = lax.axis_index("chan")
    tm_index = lax.axis_index("tm")
    first_channel = chan_index * channel_count
    local_flags = lax.dynamic_slice_in_dim(channel_flags, first_channel, channel_count, 0)
    spectrum, baseline_stats = spectrum_terms(
        summed, first_channel, local_flags.astype(jnp.float32)
    )
    block_pairs = spectrum.shape[0]
    total_time = voltages.shape[0] * tm_size
    norm_factor = 1.0 / math.sqrt(CHANNELS * total_time)
    spectrum = lax.psum_scatter(
        spectrum.reshape(block_pairs // 2, -1, DEPTH), "chan", scatter_dimension=0, tiled=True
    )
    own_pairs = block_pairs // chan_size
    rm_spectrum = (spectrum * norm_factor).reshape(1, own_pairs, window, 2, DEPTH)
    all_stats = lax.all_gather(
        lax.psum(baseline_stats, "chan"), "tm", axis=0, tiled=True
    ) / CHANNELS
    station_axis = jnp.arange(stations, dtype=jnp.int32)
    window_map = (window_stations[:, None] == station_axis[None, :]).astype(jnp.float32)
    station_map = jnp.eye(stations, dtype=jnp.float32)
    leak_real = jnp.zeros((stations,), jnp.float32)
    leak_imag = jnp.zeros((stations,), jnp.float32)
    fields = [all_stats[:, :, column] for column in range(8)]
    for iteration in range(ITERATIONS):
        numer_real, numer_imag, weight_sum = station_terms(
            leak_real, leak_imag, fields, station_map, window_map
        )
        leak_real = numer_real / (weight_sum + 1e-06)
        leak_imag = numer_imag / (weight_sum + 1e-06)
    return (rm_spectrum, jnp.stack([leak_real, leak_imag], 0))


def solution(mesh):
    return jax.shard_map(
        per_device,
        mesh=mesh,
        in_specs=(P("tm", "chan", None, None), P(), P()),
        out_specs=(P("tm", "chan", None, None, None), P()),
        check_vma=False,
    )
```

```python
import math

import jax
import jax.numpy as jnp
from jax import lax
from jax.sharding import Mesh, PartitionSpec as P

CHANNELS = 8192
DEPTH = 1024
ITERATIONS = 3
CHAN = ("chan_outer", "chan_inner")


def phase_table(first_channel, channel_count):
    chan_pos = (first_channel + jnp.arange(channel_count, dtype=jnp.int32)).astype(jnp.float32)
    frequency = 1.0 + (chan_pos + 0.5) / CHANNELS
    lambda_sq = 1.0 / (frequency * frequency)
    depth_grid = (jnp.arange(DEPTH).astype(jnp.float32) - DEPTH // 2) * 2.0
    angles = 2.0 * depth_grid[None, :] * (lambda_sq[:, None] - 0.5)
    return (jnp.cos(angles).astype(jnp.bfloat16), jnp.sin(angles).astype(jnp.bfloat16))


def station_terms(leak_real, leak_imag, fields, station_map, window_map):
    far_real = jnp.sum(station_map * leak_real[None, :], 1)[:, None]
    far_imag = jnp.sum(station_map * leak_imag[None, :], 1)[:, None]
    near_real = jnp.sum(window_map * leak_real[None, :], 1)[None, :]
    near_imag = jnp.sum(window_map * leak_imag[None, :], 1)[None, :]
    row_real = fields[0] - (far_real * fields[2] + far_imag * fields[3])
    row_imag = fields[1] - (far_real * fields[3] - far_imag * fields[2])
    col_real = fields[4] - (near_real * fields[2] + near_imag * fields[3])
    col_imag = -(fields[5] - (near_imag * fields[2] - near_real * fields[3]))
    numer_real = jnp.sum(window_map * jnp.sum(row_real, 0)[:, None], 0) + jnp.sum(
        station_map * jnp.sum(col_real, 1)[:, None], 0
    )
    numer_imag = jnp.sum(window_map * jnp.sum(row_imag, 0)[:, None], 0) + jnp.sum(
        station_map * jnp.sum(col_imag, 1)[:, None], 0
    )
    weight_sum = jnp.sum(window_map * jnp.sum(fields[6], 0)[:, None], 0) + jnp.sum(
        station_map * jnp.sum(fields[7], 1)[:, None], 0
    )
    return (numer_real, numer_imag, weight_sum)


def spectrum_terms(local_vis, first_channel, flag_weights):
    pairs = local_vis.shape[0] // 2
    window = local_vis.shape[2] // 2
    channel_count = local_vis.shape[3]
    six = local_vis.reshape(pairs, 2, 2, window, 2, channel_count)

    def correlation(feed_a, feed_b):
        return six[:, feed_b, :, :, feed_a, :].astype(jnp.float32)

    corr_xx = correlation(0, 0)
    corr_xy = correlation(0, 1)
    corr_yx = correlation(1, 0)
    corr_yy = correlation(1, 1)
    pol_real = 0.5 * (corr_xx[:, 0] - corr_yy[:, 0]) - 0.5 * (corr_xy[:, 1] + corr_yx[:, 1])
    pol_imag = 0.5 * (corr_xx[:, 1] - corr_yy[:, 1]) + 0.5 * (corr_xy[:, 0] + corr_yx[:, 0])
    pol_real = (pol_real * flag_weights).astype(jnp.bfloat16).reshape(pairs * window, channel_count)
    pol_imag = (pol_imag * flag_weights).astype(jnp.bfloat16).reshape(pairs * window, channel_count)

    def conj_sum(left, right):
        real_part = jnp.sum(
            flag_weights * (left[:, 0] * right[:, 0] + left[:, 1] * right[:, 1]), -1
        )
        imag_part = jnp.sum(
            flag_weights * (left[:, 1] * right[:, 0] - left[:, 0] * right[:, 1]), -1
        )
        return (real_part, imag_part)

    cross_real, cross_imag = conj_sum(corr_xy, corr_yy)
    mixed_real, mixed_imag = conj_sum(corr_xx, corr_yy)
    side_real, side_imag = conj_sum(corr_xy, corr_xx)
    power_y = jnp.sum(
        flag_weights * (corr_yy[:, 0] * corr_yy[:, 0] + corr_yy[:, 1] * corr_yy[:, 1]), -1
    )
    power_x = jnp.sum(
        flag_weights * (corr_xx[:, 0] * corr_xx[:, 0] + corr_xx[:, 1] * corr_xx[:, 1]), -1
    )
    baseline_stats = jnp.stack(
        [cross_real, cross_imag, mixed_real, mixed_imag, side_real, side_imag, power_y, power_x], -1
    )
    block_width = math.gcd(channel_count, 1024)

    def add_block(block_id, total):
        offset = block_id * block_width
        cosine, sine_part = phase_table(first_channel + offset, block_width)
        left = jnp.concatenate(
            [
                lax.dynamic_slice_in_dim(pol_real, offset, block_width, 1),
                lax.dynamic_slice_in_dim(pol_imag, offset, block_width, 1),
            ],
            1,
        )
        right = jnp.concatenate(
            [jnp.concatenate([cosine, -sine_part], 1), jnp.concatenate([sine_part, cosine], 1)], 0
        )
        return total + jnp.dot(left, right, preferred_element_type=jnp.float32)

    total = lax.fori_loop(
        0,
        channel_count // block_width,
        add_block,
        jnp.zeros((pairs * window, 2 * DEPTH), jnp.float32),
    )
    return (total.reshape(pairs, window, 2 * DEPTH), baseline_stats)


def per_device(voltages, window_stations, channel_flags):
    tm_size = lax.axis_size("tm")
    chan_size = lax.axis_size(CHAN)
    inputs = voltages.shape[3]
    stations = inputs // 2
    window = window_stations.shape[0]
    channel_count = voltages.shape[1]
    feed_index = (2 * window_stations[:, None] + jnp.arange(2, dtype=jnp.int32)[None, :]).reshape(
        -1
    )
    onehot = (
        jnp.arange(inputs, dtype=jnp.int32)[:, None] == feed_index[None, :]
    ).astype(jnp.float32)
    zero = jnp.zeros_like(onehot)
    selector = jnp.stack(
        [
            jnp.stack([jnp.stack([onehot, zero], 1), jnp.stack([zero, -onehot], 1)], 1),
            jnp.stack([jnp.stack([zero, onehot], 1), jnp.stack([onehot, zero], 1)], 1),
        ],
        0,
    ).reshape(2, inputs, 2, -1).astype(voltages.dtype)
    left = jnp.einsum(
        "tcsi,sirq->tcrq", voltages, selector, preferred_element_type=jnp.float32
    ).astype(voltages.dtype)
    partial = jnp.einsum(
        "tcrq,tcri->iqc", left, voltages, preferred_element_type=jnp.float32
    ).astype(jnp.bfloat16)
    partial_shape = (inputs, 2, 2 * window, channel_count)
    summed = lax.psum_scatter(
        partial,
        "tm",
        scatter_dimension=0,
        tiled=True,
    ).reshape(-1, *partial_shape[1:])
    chan_index = lax.axis_index(CHAN)
    tm_index = lax.axis_index("tm")
    first_channel = chan_index * channel_count
    local_flags = lax.dynamic_slice_in_dim(channel_flags, first_channel, channel_count, 0)
    spectrum, baseline_stats = spectrum_terms(
        summed, first_channel, local_flags.astype(jnp.float32)
    )
    block_pairs = spectrum.shape[0]
    total_time = voltages.shape[0] * tm_size
    norm_factor = 1.0 / math.sqrt(CHANNELS * total_time)
    outer = lax.axis_size("chan_outer")
    inner = lax.axis_size("chan_inner")
    spectrum = spectrum.reshape(outer, inner, -1, DEPTH)
    spectrum = jnp.swapaxes(spectrum, 0, 1).reshape(outer * inner, -1, DEPTH)
    spectrum = lax.psum_scatter(spectrum, "chan_inner", scatter_dimension=0, tiled=True)
    spectrum = lax.psum_scatter(spectrum, "chan_outer", scatter_dimension=0, tiled=True)
    own_pairs = block_pairs // chan_size
    rm_spectrum = (spectrum * norm_factor).reshape(1, own_pairs, window, 2, DEPTH)
    all_stats = lax.all_gather(
        lax.psum(baseline_stats, CHAN), "tm", axis=0, tiled=True
    ) / CHANNELS
    station_axis = jnp.arange(stations, dtype=jnp.int32)
    window_map = (window_stations[:, None] == station_axis[None, :]).astype(jnp.float32)
    station_map = jnp.eye(stations, dtype=jnp.float32)
    leak_real = jnp.zeros((stations,), jnp.float32)
    leak_imag = jnp.zeros((stations,), jnp.float32)
    fields = [all_stats[:, :, column] for column in range(8)]
    for iteration in range(ITERATIONS):
        numer_real, numer_imag, weight_sum = station_terms(
            leak_real, leak_imag, fields, station_map, window_map
        )
        leak_real = numer_real / (weight_sum + 1e-06)
        leak_imag = numer_imag / (weight_sum + 1e-06)
    return (rm_spectrum, jnp.stack([leak_real, leak_imag], 0))


def solution(mesh):
    chan_size, tm_size = mesh.devices.shape
    inner = 2 if chan_size % 2 == 0 else 1
    split_mesh = Mesh(
        mesh.devices.reshape(chan_size // inner, inner, tm_size),
        ("chan_outer", "chan_inner", "tm"),
    )
    return jax.shard_map(
        per_device,
        mesh=split_mesh,
        in_specs=(P("tm", CHAN, None, None), P(), P()),
        out_specs=(P("tm", CHAN, None, None, None), P()),
        check_vma=False,
    )
```
